768 devices in a mesh: seq: 24 (over z, core), head: 32 (over x, y).
Axes of the slice: x: 4, y: 8, z: 12, core: 2. Of those that a mesh axis runs over, the one named last changes fastest.
Arguments:
- queries: bfloat16 [32, 12288, 128], P('head', 'seq'), may hold values from -120 to 120
- keys: bfloat16 [32, 12288, 128], P('head', 'seq'), may hold values from -4.5 to 4.5
- values: bfloat16 [32, 12288, 128], P('head', 'seq'), may hold values from -6 to 6
- grad_out: bfloat16 [32, 12288, 128], P('head', 'seq'), may hold values from -6 to 6
- rand_owner: int32 [192, 3], replicated, may hold values from 0 to 23, all different within a row; in each aligned block of 8 rows (0 to 7, 8 to 15, ...) at most 2 rows name the same one
- rand_slot: int32 [192, 3], replicated, may hold values from 0 to 7
- glob_ids: int32 [2], replicated, may hold values from 0 to 7, as said below
Outputs:
- grad_q: bfloat16 [32, 12288, 128], P('head', 'seq')
- grad_k: bfloat16 [32, 12288, 128], P('head', 'seq')
- grad_v: bfloat16 [32, 12288, 128], P('head', 'seq')
The draws below stay inside these ranges and needn't reach their ends.
Inputs may be any that keep to these rules, and one draw needn't show every extreme that they name: `rand_owner`: in the 8 rows of one device, each row names 3 different seq indices and no index is named more than 2 times; some index is named exactly 2 times. `glob_ids`: 2 different block numbers; the first device's last block is always one of them.
All inputs are finite; a program needn't handle non-finite values.
Results may differ from the reference program's by a relative error of at most 0.022.
Values may be sent and summed in bfloat16 or wider, within the bound.
No kernel may reach another device: no remote copies, remote signals or barrier semaphores. Data moves between devices by JAX's collectives and lax.ppermute only.
A program may use at most 32 MiB of HBM per device.

```python
import math
import jax
import jax.numpy as jnp
import numpy as np
from jax import lax

HEAD_DIM = 128
BLOCK = 64
RAND = 3
GLOB = 2
QB_DEV = 8
HEADS = 32
NB = 192
TOKENS = 12288
CAP = 2
N_SEQ = 24


def shared_keys(key):
    drawn = jax.random.normal(jax.random.fold_in(key, 101), (HEADS, TOKENS, HEAD_DIM), jnp.float32)
    return jnp.clip(drawn, -4.0, 4.0)


def draw_keys(key, part):
    base_rows = shared_keys(key)
    return base_rows.astype(jnp.bfloat16)


def draw_queries(key, part):
    drawn = jnp.clip(jax.random.normal(jax.random.fold_in(key, 103), (HEADS, TOKENS, HEAD_DIM), jnp.float32), -4.0, 4.0)
    return drawn.astype(jnp.bfloat16)


def draw_glob_ids(key, part):
    others = jax.random.permutation(jax.random.fold_in(key, 105), QB_DEV - 1)[:GLOB - 1].astype(jnp.int32)
    chosen = jnp.concatenate([others, jnp.full((1,), QB_DEV - 1, jnp.int32)])
    order = jax.random.permutation(jax.random.fold_in(key, 106), GLOB)
    return chosen[order].astype(jnp.int32)


def touch_ends(values, rng, low, largest):
    longest = values.shape.index(max(values.shape))
    spots = []
    for shift in (0, 1):
        where = [jax.random.randint(jax.random.fold_in(rng, axis), (), 0, length) for axis, length in enumerate(values.shape)]
        where[longest] = (where[longest] + shift) % values.shape[longest]
        spots.append(tuple(where))
    return values.at[spots[0]].set(low).at[spots[1]].set(largest)


def levels(rng, dims, shards, least, high):
    def one(axis_at, parts):
        heights = jax.random.uniform(jax.random.fold_in(jax.random.fold_in(rng, 6), axis_at), (parts,), jnp.float32, least / len(shards), high / len(shards))
        return jnp.repeat(jnp.exp(heights), dims[axis_at] // parts).reshape((-1,) + (1,) * (len(dims) - axis_at - 1))

    gain = one(*shards[0])
    for cut in shards[1:]:
        gain = gain * one(*cut)
    return gain


def shared_out(rng, own, number, rows, amount, top, most, skew):
    ranking = jax.random.permutation(rng, amount)
    heavy_load, ordinary = portions_of(amount, rows * top, most, skew, True), portions_of(amount, rows * top, most, skew, False)
    places = jnp.arange(amount)

    def named(sizes, offset_by):
        used = int((sizes > 0).sum())
        fixed = max(1, used // 4)
        passed = fixed + (places - fixed + offset_by * (used - fixed)) % max(1, amount - fixed)
        return jnp.zeros((amount,), jnp.int32).at[ranking[jnp.where(places < fixed, places, passed)]].set(jnp.asarray(sizes, jnp.int32))

    sizes = jnp.where(number % 4 == 0, named(heavy_load, number // 4), named(ordinary, number - number // 4 - 1))
    mixed = jax.random.permutation(jax.random.fold_in(own, 3), amount)
    donor, sink = mixed[0:amount // 2 * 2:2], mixed[1:amount // 2 * 2:2]
    slack = jnp.minimum(sizes[donor] - 1, most - sizes[sink]) // 2
    slack = jnp.where((donor == ranking[0]) | (sink == ranking[0]) | (sizes[sink] == 0), 0, jnp.maximum(slack, 0))
    passed = jax.random.randint(jax.random.fold_in(own, 4), (amount // 2,), 0, 1 << 20) % (slack + 1)
    sizes = sizes.at[donor].add(-passed).at[sink].add(passed)
    items = jnp.searchsorted(jnp.cumsum(sizes), jnp.arange(rows * top), side="right").astype(jnp.int32)
    listing = items.reshape(top, rows).T
    listing = listing[jax.random.permutation(jax.random.fold_in(own, 1), rows)]
    offset_by = jax.random.randint(jax.random.fold_in(own, 2), (rows, 1), 0, top)
    return jnp.take_along_axis(listing, (jnp.arange(top)[None, :] + offset_by) % top, axis=1)


def portions_of(number_of, total, limit, slope, full):
    loads = [(1 << 20) // math.isqrt(rank ** slope) + 1 for rank in range(1, number_of + 1)]
    largest = limit if full else min(limit, max(-(-total // number_of), total * loads[0] // sum(loads)))
    least = 1 if total - largest >= number_of - 1 else 0
    given, rest = [largest] + [least] * (number_of - 1), total - largest - least * (number_of - 1)
    while rest > 0:
        movable = [i for i in range(1, number_of) if given[i] < largest] or [i for i in range(1, number_of) if given[i] < limit]
        whole, budget = sum([loads[i] for i in movable]), rest
        for i in movable:
            more = min(limit - given[i], max(1, budget * loads[i] // whole), rest)
            given[i] = given[i] + more
            rest = rest - more
    return np.array(given)


def bell_draw(own_key, extent, spread, reach, pieces=(), held_as=jnp.bfloat16):
    factor_of = levels(own_key, extent, pieces, -0.22, 0.18) if pieces else 1.0
    entries = jax.random.normal(own_key, extent, jnp.float32) * spread * factor_of
    return jnp.minimum(jnp.maximum(entries, -reach), reach).astype(held_as)


def setup_inputs(seed: int = 0) -> dict:
    seeds = jax.random.split(jax.random.key(seed), 8)
    queries = draw_queries(jax.random.fold_in(seeds[7], 71), 0)
    keys = draw_keys(jax.random.fold_in(seeds[7], 71), 0)
    values = bell_draw(seeds[2], (HEADS, TOKENS, HEAD_DIM), 1.0, 6.0, ((0, 32), (1, 24)))
    grad_out = bell_draw(seeds[3], (HEADS, TOKENS, HEAD_DIM), 1.0, 6.0, ((0, 32), (1, 24)))
    rand_owner_keys = jax.random.split(jax.random.fold_in(seeds[4], 1), NB // QB_DEV)
    rand_owner_turns = jax.random.permutation(jax.random.fold_in(seeds[4], 3), NB // QB_DEV)
    rand_owner = jax.vmap(lambda own, number: shared_out(jax.random.fold_in(seeds[4], 2), own, number, QB_DEV, N_SEQ, RAND, CAP, 2))(rand_owner_keys, rand_owner_turns).reshape((NB, RAND))
    rand_slot = touch_ends(jax.random.randint(seeds[5], (NB, RAND), 0, QB_DEV), jax.random.fold_in(seeds[5], 1), 0, QB_DEV - 1).astype(jnp.int32)
    glob_ids = draw_glob_ids(jax.random.fold_in(seeds[7], 71), 0)
    return {"queries": queries, "keys": keys, "values": values, "grad_out": grad_out, "rand_owner": rand_owner, "rand_slot": rand_slot, "glob_ids": glob_ids}


NEG_FILL = -1.0e30


def round_trip(tensor):
    return lax.optimization_barrier(tensor.astype(jnp.bfloat16)).astype(jnp.float32)


def one_head(head_args, rand_owner, rand_slot, glob_ids):
    query, key_rows, value_rows, cotan = head_args
    score_scale = 1.0 / (HEAD_DIM ** 0.5)
    query_f32 = query.reshape(NB, BLOCK, HEAD_DIM).astype(jnp.float32)
    cotan_f32 = cotan.reshape(NB, BLOCK, HEAD_DIM).astype(jnp.float32)
    pair_blocks = jnp.concatenate([key_rows, value_rows], axis=1).reshape(NB, BLOCK, 2 * HEAD_DIM)
    block_index = jnp.arange(NB, dtype=jnp.int32)
    window = block_index[:, None] + jnp.arange(-1, 2, dtype=jnp.int32)[None, :]
    window_ok = (window >= 0) & (window < NB)
    window_at = jnp.clip(window, 0, NB - 1).astype(jnp.int32)
    random_at = (rand_owner * QB_DEV + rand_slot).astype(jnp.int32)
    global_at = jnp.broadcast_to(glob_ids[None, :], (NB, GLOB)).astype(jnp.int32)
    key_table = jnp.concatenate([window_at, random_at, global_at], axis=1)
    key_valid = jnp.concatenate([window_ok, jnp.ones((NB, RAND + GLOB), dtype=bool)], axis=1)
    picked = pair_blocks[key_table]
    key_sel = picked[..., :HEAD_DIM].astype(jnp.float32)
    value_sel = picked[..., HEAD_DIM:].astype(jnp.float32)
    scores = jnp.einsum("iqd,iskd->iqsk", query_f32, key_sel) * score_scale
    scores = jnp.where(key_valid[:, None, :, None], scores, NEG_FILL)
    row_max = jnp.max(scores, axis=(2, 3), keepdims=True)
    expo_terms = jnp.exp(scores - row_max)
    weights = expo_terms / jnp.sum(expo_terms, axis=(2, 3), keepdims=True)
    weights_low = round_trip(weights)
    attended = jnp.einsum("iqsk,iskd->iqd", weights_low, value_sel)
    delta = jnp.sum(cotan_f32 * attended, axis=2)
    grad_values = jnp.einsum("iqsk,iqd->iskd", weights_low, cotan_f32)
    grad_weights = jnp.einsum("iqd,iskd->iqsk", cotan_f32, value_sel)
    grad_scores = round_trip(weights * (grad_weights - delta[:, :, None, None]))
    grad_query = jnp.einsum("iqsk,iskd->iqd", grad_scores, key_sel) * score_scale
    grad_keys = jnp.einsum("iqsk,iqd->iskd", grad_scores, query_f32) * score_scale
    contrib = jnp.concatenate([grad_keys, grad_values], axis=3)
    accum = jnp.zeros((NB, BLOCK, 2 * HEAD_DIM), jnp.float32)
    query_owner = block_index // QB_DEV
    for window_slot in range(3):
        crossing = window_ok[:, window_slot] & (window_at[:, window_slot] // QB_DEV != query_owner)
        term_now = contrib[:, window_slot]
        term_now = jnp.where(crossing[:, None, None], round_trip(term_now), term_now)
        accum = accum.at[window_at[:, window_slot]].add(term_now)
    for rand_index in range(RAND):
        accum = accum.at[random_at[:, rand_index]].add(round_trip(contrib[:, 3 + rand_index]))
    for glob_index in range(GLOB):
        partial_value = jnp.sum(contrib[:, 3 + RAND + glob_index].reshape(N_SEQ, QB_DEV, BLOCK, 2 * HEAD_DIM), axis=1)
        accum = accum.at[glob_ids[glob_index]].add(jnp.sum(round_trip(partial_value), axis=0))
    grad_q = grad_query.reshape(TOKENS, HEAD_DIM).astype(jnp.bfloat16)
    grad_k = accum[..., :HEAD_DIM].reshape(TOKENS, HEAD_DIM).astype(jnp.bfloat16)
    grad_v = accum[..., HEAD_DIM:].reshape(TOKENS, HEAD_DIM).astype(jnp.bfloat16)
    return grad_q, grad_k, grad_v


def reference(queries, keys, values, grad_out, rand_owner, rand_slot, glob_ids):
    def per_head(head_args):
        return one_head(head_args, rand_owner, rand_slot, glob_ids)

    grad_q, grad_k, grad_v = lax.map(per_head, (queries, keys, values, grad_out))
    return grad_q, grad_k, grad_v
```

```python
import math

import jax
import jax.numpy as jnp
from jax import lax
from jax.sharding import PartitionSpec as P

BLOCK = 64


NEG_FILL = -1e30


def padded(array, sides, width):
    for axis, dim in sides:
        devices, length = (lax.axis_size(axis), array.shape[dim])
        up = [(i, (i + 1) % devices) for i in range(devices - 1)]
        down = [(j, i) for i, j in up]
        last = lax.slice_in_dim(array, length - width, length, axis=dim)
        first = lax.slice_in_dim(array, 0, width, axis=dim)
        before = lax.ppermute(last, axis, up)
        after = lax.ppermute(first, axis, down)
        array = jnp.concatenate([before, array, after], axis=dim)
    return array


def from_root(block, axis, source):
    block = jnp.where(lax.axis_index(axis) == source, block, jnp.zeros_like(block))
    return lax.psum(block, axis)


def block_edges(tensor):
    return padded(tensor, (("seq", 1),), BLOCK)


def local(queries, keys, values, grad_out, rand_owner, rand_slot, glob_ids):
    head_count, row_count, head_width = queries.shape
    block_count = row_count // BLOCK
    rand_count = rand_owner.shape[1]
    glob_count = glob_ids.shape[0]
    seq_count = lax.axis_size("seq")
    seq_place = lax.axis_index("seq")
    slot_count = min(
        block_count, max(2, (2 * block_count * rand_count + seq_count - 1) // seq_count)
    )
    pair_width = 2 * head_width
    score_scale = 1.0 / math.sqrt(head_width)
    paired = jnp.concatenate([keys, values], axis=2)
    paired_blocks = paired.reshape(head_count, block_count, BLOCK, pair_width)
    widened = block_edges(paired).reshape(head_count, block_count + 2, BLOCK, pair_width)
    window_pairs = jnp.stack(
        [widened[:, offset : offset + block_count] for offset in range(3)], axis=2
    )
    global_block = seq_place * block_count + jnp.arange(block_count, dtype=jnp.int32)
    window_ids = global_block[:, None] + jnp.arange(-1, 2, dtype=jnp.int32)[None, :]
    window_ok = (window_ids >= 0) & (window_ids < seq_count * block_count)
    owners_all = rand_owner.reshape(seq_count, block_count * rand_count)
    slots_all = rand_slot.reshape(seq_count, block_count * rand_count)
    owner_hot = (
        owners_all[:, :, None] == jnp.arange(seq_count, dtype=jnp.int32)[None, None, :]
    ).astype(jnp.int32)
    before = jnp.cumsum(owner_hot, axis=1) - owner_hot
    position = jnp.sum(before * owner_hot, axis=2)
    to_here = owners_all == seq_place
    slot_hot = (
        position[:, :, None] == jnp.arange(slot_count, dtype=jnp.int32)[None, None, :]
    ) & to_here[:, :, None]
    send_block = jnp.sum(slot_hot.astype(jnp.int32) * slots_all[:, :, None], axis=1)
    send_used = jnp.any(slot_hot, axis=1)
    my_owner = lax.dynamic_index_in_dim(owners_all, seq_place, 0, keepdims=False)
    my_slot = lax.dynamic_index_in_dim(slots_all, seq_place, 0, keepdims=False)
    my_position = lax.dynamic_index_in_dim(position, seq_place, 0, keepdims=False)
    return_at = my_owner * slot_count + my_position
    wanted = my_owner * block_count + my_slot
    empty_pairs = jnp.zeros((head_count, block_count * rand_count, BLOCK, pair_width), jnp.bfloat16)
    piece_rows = lax.all_gather(paired, "seq", axis=1, tiled=True)
    piece_blocks = piece_rows.shape[1] // BLOCK
    grouped = piece_rows.reshape(head_count, piece_blocks, BLOCK, pair_width)
    inside = (wanted >= 0) & (wanted < piece_blocks)
    taken = jnp.take(grouped, jnp.clip(wanted, 0, piece_blocks - 1), axis=1)
    random_pairs = jnp.where(inside[None, :, None, None], taken, empty_pairs)
    random_pairs = random_pairs.reshape(head_count, block_count, rand_count, BLOCK, pair_width)
    global_pairs = jnp.take(grouped, glob_ids, axis=1)
    global_wide = jnp.broadcast_to(
        global_pairs[:, None], (head_count, block_count, glob_count, BLOCK, pair_width)
    )
    key_pairs = jnp.concatenate([window_pairs, random_pairs, global_wide], axis=2)
    key_part = key_pairs[..., :head_width]
    value_part = key_pairs[..., head_width:]
    key_valid = jnp.concatenate(
        [window_ok, jnp.ones((block_count, rand_count + glob_count), dtype=bool)], axis=1
    )
    query_blocks = queries.reshape(head_count, block_count, BLOCK, head_width)
    cotan_blocks = grad_out.reshape(head_count, block_count, BLOCK, head_width)
    scores = (
        jnp.einsum("hiqd,hiskd->hiqsk", query_blocks, key_part, preferred_element_type=jnp.float32)
        * score_scale
    )
    scores = jnp.where(key_valid[None, :, None, :, None], scores, NEG_FILL)
    row_max = jnp.max(scores, axis=(3, 4), keepdims=True)
    expo_terms = jnp.exp(scores - row_max)
    weights = expo_terms / jnp.sum(expo_terms, axis=(3, 4), keepdims=True)
    weights_low = weights.astype(jnp.bfloat16)
    attended = jnp.einsum(
        "hiqsk,hiskd->hiqd", weights_low, value_part, preferred_element_type=jnp.float32
    )
    delta = jnp.sum(cotan_blocks.astype(jnp.float32) * attended, axis=3)
    grad_values = jnp.einsum(
        "hiqsk,hiqd->hiskd", weights_low, cotan_blocks, preferred_element_type=jnp.float32
    )
    grad_weights = jnp.einsum(
        "hiqd,hiskd->hiqsk", cotan_blocks, value_part, preferred_element_type=jnp.float32
    )
    grad_scores = (weights * (grad_weights - delta[:, :, :, None, None])).astype(jnp.bfloat16)
    grad_query = (
        jnp.einsum("hiqsk,hiskd->hiqd", grad_scores, key_part, preferred_element_type=jnp.float32)
        * score_scale
    )
    grad_keys = (
        jnp.einsum(
            "hiqsk,hiqd->hiskd", grad_scores, query_blocks, preferred_element_type=jnp.float32
        )
        * score_scale
    )
    contrib = jnp.concatenate([grad_keys, grad_values], axis=4)
    wide_grad = jnp.pad(contrib[:, :, 0], ((0, 0), (0, 2), (0, 0), (0, 0)))
    for offset in range(1, 3):
        wide_grad = wide_grad + jnp.pad(
            contrib[:, :, offset], ((0, 0), (offset, 2 - offset), (0, 0), (0, 0))
        )
    edge_out = jnp.concatenate([wide_grad[:, 0], wide_grad[:, block_count + 1]], axis=1).astype(
        jnp.bfloat16
    )
    edge_in = block_edges(edge_out)
    from_left = edge_in[:, :BLOCK].astype(jnp.float32)
    from_right = edge_in[:, 3 * BLOCK :].astype(jnp.float32)
    accum = wide_grad[:, 1 : block_count + 1]
    accum = accum.at[:, 0].add(from_left)
    accum = accum.at[:, block_count - 1].add(from_right)
    random_terms = contrib[:, :, 3 : 3 + rand_count].astype(jnp.bfloat16)
    random_terms = random_terms.reshape(head_count, block_count * rand_count, BLOCK, pair_width)
    outgoing_grads = jnp.zeros(
        (head_count, seq_count * slot_count, BLOCK, pair_width), jnp.bfloat16
    )
    outgoing_grads = outgoing_grads.at[:, return_at].set(random_terms)
    outgoing_grads = outgoing_grads.reshape(head_count, seq_count, slot_count, BLOCK, pair_width)
    returned = lax.all_to_all(outgoing_grads, "seq", split_axis=1, concat_axis=1, tiled=True)
    returned = returned.reshape(head_count, seq_count * slot_count, BLOCK * pair_width)
    block_hot = (
        send_block.reshape(-1)[:, None] == jnp.arange(block_count, dtype=jnp.int32)[None, :]
    ) & send_used.reshape(-1)[:, None]
    gathered = jnp.einsum(
        "cb,ecx->ebx", block_hot.astype(jnp.bfloat16), returned, preferred_element_type=jnp.float32
    )
    accum = accum + gathered.reshape(head_count, block_count, BLOCK, pair_width)
    global_terms = jnp.sum(contrib[:, :, 3 + rand_count :], axis=1)
    global_parts = lax.all_gather(global_terms.astype(jnp.bfloat16), "seq", axis=0)
    global_sums = jnp.sum(global_parts.astype(jnp.float32), axis=0)
    at_first = (seq_place == 0).astype(jnp.float32)
    accum = accum.at[:, glob_ids].add(global_sums * at_first)
    grad_q = grad_query.reshape(head_count, row_count, head_width).astype(jnp.bfloat16)
    grad_k = accum[..., :head_width].reshape(head_count, row_count, head_width).astype(jnp.bfloat16)
    grad_v = accum[..., head_width:].reshape(head_count, row_count, head_width).astype(jnp.bfloat16)
    return (grad_q, grad_k, grad_v)


def solution(mesh):
    return jax.shard_map(
        local,
        mesh=mesh,
        in_specs=(
            P("head", "seq", None),
            P("head", "seq", None),
            P("head", "seq", None),
            P("head", "seq", None),
            P(),
            P(),
            P(),
        ),
        out_specs=(P("head", "seq", None), P("head", "seq", None), P("head", "seq", None)),
        check_vma=False,
    )
```

```python
import math

import jax
import jax.numpy as jnp
from jax import lax
from jax.sharding import PartitionSpec as P

BLOCK = 64


NEG_FILL = -1e30


def local(queries, keys, values, grad_out, rand_owner, rand_slot, glob_ids):
    head_count, row_count, head_width = queries.shape
    block_count = row_count // BLOCK
    rand_count = rand_owner.shape[1]
    glob_count = glob_ids.shape[0]
    seq_count = lax.axis_size("seq")
    seq_place = lax.axis_index("seq")
    slot_count = min(
        block_count, max(2, (2 * block_count * rand_count + seq_count - 1) // seq_count)
    )
    pair_width = 2 * head_width
    score_scale = 1.0 / math.sqrt(head_width)
    paired = jnp.concatenate([keys, values], axis=2)
    paired_blocks = paired.reshape(head_count, block_count, BLOCK, pair_width)
    piece_rows = lax.all_gather(paired, "seq", axis=1, tiled=True)
    row_start = seq_place * row_count
    edge_before = lax.dynamic_slice_in_dim(piece_rows, row_start - BLOCK, BLOCK, axis=1)
    edge_after = lax.dynamic_slice_in_dim(piece_rows, row_start + row_count, BLOCK, axis=1)
    widened = jnp.concatenate([edge_before, paired, edge_after], axis=1)
    widened = widened.reshape(head_count, block_count + 2, BLOCK, pair_width)
    window_pairs = jnp.stack(
        [widened[:, offset : offset + block_count] for offset in range(3)], axis=2
    )
    global_block = seq_place * block_count + jnp.arange(block_count, dtype=jnp.int32)
    window_ids = global_block[:, None] + jnp.arange(-1, 2, dtype=jnp.int32)[None, :]
    window_ok = (window_ids >= 0) & (window_ids < seq_count * block_count)
    owners_all = rand_owner.reshape(seq_count, block_count * rand_count)
    slots_all = rand_slot.reshape(seq_count, block_count * rand_count)
    owner_hot = (
        owners_all[:, :, None] == jnp.arange(seq_count, dtype=jnp.int32)[None, None, :]
    ).astype(jnp.int32)
    before = jnp.cumsum(owner_hot, axis=1) - owner_hot
    position = jnp.sum(before * owner_hot, axis=2)
    to_here = owners_all == seq_place
    slot_hot = (
        position[:, :, None] == jnp.arange(slot_count, dtype=jnp.int32)[None, None, :]
    ) & to_here[:, :, None]
    send_block = jnp.sum(slot_hot.astype(jnp.int32) * slots_all[:, :, None], axis=1)
    send_used = jnp.any(slot_hot, axis=1)
    my_owner = lax.dynamic_index_in_dim(owners_all, seq_place, 0, keepdims=False)
    my_slot = lax.dynamic_index_in_dim(slots_all, seq_place, 0, keepdims=False)
    my_position = lax.dynamic_index_in_dim(position, seq_place, 0, keepdims=False)
    return_at = my_owner * slot_count + my_position
    wanted = my_owner * block_count + my_slot
    empty_pairs = jnp.zeros((head_count, block_count * rand_count, BLOCK, pair_width), jnp.bfloat16)
    piece_blocks = piece_rows.shape[1] // BLOCK
    grouped = piece_rows.reshape(head_count, piece_blocks, BLOCK, pair_width)
    inside = (wanted >= 0) & (wanted < piece_blocks)
    taken = jnp.take(grouped, jnp.clip(wanted, 0, piece_blocks - 1), axis=1)
    random_pairs = jnp.where(inside[None, :, None, None], taken, empty_pairs)
    random_pairs = random_pairs.reshape(head_count, block_count, rand_count, BLOCK, pair_width)
    global_pairs = jnp.take(grouped, glob_ids, axis=1)
    global_wide = jnp.broadcast_to(
        global_pairs[:, None], (head_count, block_count, glob_count, BLOCK, pair_width)
    )
    key_pairs = jnp.concatenate([window_pairs, random_pairs, global_wide], axis=2)
    key_part = key_pairs[..., :head_width]
    value_part = key_pairs[..., head_width:]
    key_valid = jnp.concatenate(
        [window_ok, jnp.ones((block_count, rand_count + glob_count), dtype=bool)], axis=1
    )
    query_blocks = queries.reshape(head_count, block_count, BLOCK, head_width)
    cotan_blocks = grad_out.reshape(head_count, block_count, BLOCK, head_width)
    scores = (
        jnp.einsum("hiqd,hiskd->hiqsk", query_blocks, key_part, preferred_element_type=jnp.float32)
        * score_scale
    )
    scores = jnp.where(key_valid[None, :, None, :, None], scores, NEG_FILL)
    row_max = jnp.max(scores, axis=(3, 4), keepdims=True)
    expo_terms = jnp.exp(scores - row_max)
    weights = expo_terms / jnp.sum(expo_terms, axis=(3, 4), keepdims=True)
    weights_low = weights.astype(jnp.bfloat16)
    attended = jnp.einsum(
        "hiqsk,hiskd->hiqd", weights_low, value_part, preferred_element_type=jnp.float32
    )
    delta = jnp.sum(cotan_blocks.astype(jnp.float32) * attended, axis=3)
    grad_values = jnp.einsum(
        "hiqsk,hiqd->hiskd", weights_low, cotan_blocks, preferred_element_type=jnp.float32
    )
    grad_weights = jnp.einsum(
        "hiqd,hiskd->hiqsk", cotan_blocks, value_part, preferred_element_type=jnp.float32
    )
    grad_scores = (weights * (grad_weights - delta[:, :, :, None, None])).astype(jnp.bfloat16)
    grad_query = (
        jnp.einsum("hiqsk,hiskd->hiqd", grad_scores, key_part, preferred_element_type=jnp.float32)
        * score_scale
    )
    grad_keys = (
        jnp.einsum(
            "hiqsk,hiqd->hiskd", grad_scores, query_blocks, preferred_element_type=jnp.float32
        )
        * score_scale
    )
    contrib = jnp.concatenate([grad_keys, grad_values], axis=4)
    wide_grad = jnp.pad(contrib[:, :, 0], ((0, 0), (0, 2), (0, 0), (0, 0)))
    for offset in range(1, 3):
        wide_grad = wide_grad + jnp.pad(
            contrib[:, :, offset], ((0, 0), (offset, 2 - offset), (0, 0), (0, 0))
        )
    edge_out = jnp.concatenate([wide_grad[:, 0], wide_grad[:, block_count + 1]], axis=1).astype(
        jnp.bfloat16
    )
    edge_out = edge_out.reshape(head_count, 2, BLOCK, pair_width)
    global_terms = jnp.sum(contrib[:, :, 3 + rand_count :], axis=1).astype(jnp.bfloat16)
    shared_out = jnp.concatenate([edge_out, global_terms], axis=1)
    shared_in = lax.all_gather(shared_out, "seq", axis=0)
    left_in = lax.dynamic_index_in_dim(shared_in, jnp.maximum(seq_place - 1, 0), 0, keepdims=False)
    right_in = lax.dynamic_index_in_dim(
        shared_in, jnp.minimum(seq_place + 1, seq_count - 1), 0, keepdims=False
    )
    from_left = jnp.where(seq_place > 0, left_in[:, 1].astype(jnp.float32), 0.0)
    from_right = jnp.where(seq_place < seq_count - 1, right_in[:, 0].astype(jnp.float32), 0.0)
    accum = wide_grad[:, 1 : block_count + 1]
    accum = accum.at[:, 0].add(from_left)
    accum = accum.at[:, block_count - 1].add(from_right)
    random_terms = contrib[:, :, 3 : 3 + rand_count].astype(jnp.bfloat16)
    random_terms = random_terms.reshape(head_count, block_count * rand_count, BLOCK, pair_width)
    outgoing_grads = jnp.zeros(
        (head_count, seq_count * slot_count, BLOCK, pair_width), jnp.bfloat16
    )
    outgoing_grads = outgoing_grads.at[:, return_at].set(random_terms)
    outgoing_grads = outgoing_grads.reshape(head_count, seq_count, slot_count, BLOCK, pair_width)
    returned = lax.all_to_all(outgoing_grads, "seq", split_axis=1, concat_axis=1, tiled=True)
    returned = returned.reshape(head_count, seq_count * slot_count, BLOCK * pair_width)
    block_hot = (
        send_block.reshape(-1)[:, None] == jnp.arange(block_count, dtype=jnp.int32)[None, :]
    ) & send_used.reshape(-1)[:, None]
    gathered = jnp.einsum(
        "cb,ecx->ebx", block_hot.astype(jnp.bfloat16), returned, preferred_element_type=jnp.float32
    )
    accum = accum + gathered.reshape(head_count, block_count, BLOCK, pair_width)
    global_sums = jnp.sum(shared_in[:, :, 2:].astype(jnp.float32), axis=0)
    at_first = (seq_place == 0).astype(jnp.float32)
    accum = accum.at[:, glob_ids].add(global_sums * at_first)
    grad_q = grad_query.reshape(head_count, row_count, head_width).astype(jnp.bfloat16)
    grad_k = accum[..., :head_width].reshape(head_count, row_count, head_width).astype(jnp.bfloat16)
    grad_v = accum[..., head_width:].reshape(head_count, row_count, head_width).astype(jnp.bfloat16)
    return (grad_q, grad_k, grad_v)


def solution(mesh):
    return jax.shard_map(
        local,
        mesh=mesh,
        in_specs=(
            P("head", "seq", None),
            P("head", "seq", None),
            P("head", "seq", None),
            P("head", "seq", None),
            P(),
            P(),
            P(),
        ),
        out_specs=(P("head", "seq", None), P("head", "seq", None), P("head", "seq", None)),
        check_vma=False,
    )
```

```python
import math

import jax
import jax.numpy as jnp
from jax import lax
from jax.sharding import PartitionSpec as P

BLOCK = 64


NEG_FILL = -1e30


def local(queries, keys, values, grad_out, rand_owner, rand_slot, glob_ids):
    head_count, row_count, head_width = queries.shape
    block_count = row_count // BLOCK
    rand_count = rand_owner.shape[1]
    glob_count = glob_ids.shape[0]
    seq_count = lax.axis_size("seq")
    seq_place = lax.axis_index("seq")
    slot_count = min(
        block_count, max(2, (2 * block_count * rand_count + seq_count - 1) // seq_count)
    )
    pair_width = 2 * head_width
    score_scale = 1.0 / math.sqrt(head_width)
    paired = jnp.concatenate([keys, values], axis=2)
    paired_blocks = paired.reshape(head_count, block_count, BLOCK, pair_width)
    piece_rows = lax.all_gather(paired, "seq", axis=1, tiled=True)
    row_start = seq_place * row_count
    edge_before = lax.dynamic_slice_in_dim(piece_rows, row_start - BLOCK, BLOCK, axis=1)
    edge_after = lax.dynamic_slice_in_dim(piece_rows, row_start + row_count, BLOCK, axis=1)
    widened = jnp.concatenate([edge_before, paired, edge_after], axis=1)
    widened = widened.reshape(head_count, block_count + 2, BLOCK, pair_width)
    window_pairs = jnp.stack(
        [widened[:, offset : offset + block_count] for offset in range(3)], axis=2
    )
    global_block = seq_place * block_count + jnp.arange(block_count, dtype=jnp.int32)
    window_ids = global_block[:, None] + jnp.arange(-1, 2, dtype=jnp.int32)[None, :]
    window_ok = (window_ids >= 0) & (window_ids < seq_count * block_count)
    owners_all = rand_owner.reshape(seq_count, block_count * rand_count)
    slots_all = rand_slot.reshape(seq_count, block_count * rand_count)
    owner_hot = (
        owners_all[:, :, None] == jnp.arange(seq_count, dtype=jnp.int32)[None, None, :]
    ).astype(jnp.int32)
    before = jnp.cumsum(owner_hot, axis=1) - owner_hot
    position = jnp.sum(before * owner_hot, axis=2)
    to_here = owners_all == seq_place
    slot_hot = (
        position[:, :, None] == jnp.arange(slot_count, dtype=jnp.int32)[None, None, :]
    ) & to_here[:, :, None]
    send_block = jnp.sum(slot_hot.astype(jnp.int32) * slots_all[:, :, None], axis=1)
    send_used = jnp.any(slot_hot, axis=1)
    my_owner = lax.dynamic_index_in_dim(owners_all, seq_place, 0, keepdims=False)
    my_slot = lax.dynamic_index_in_dim(slots_all, seq_place, 0, keepdims=False)
    my_position = lax.dynamic_index_in_dim(position, seq_place, 0, keepdims=False)
    return_at = my_owner * slot_count + my_position
    wanted = my_owner * block_count + my_slot
    piece_blocks = piece_rows.shape[1] // BLOCK
    grouped = piece_rows.reshape(head_count, piece_blocks, BLOCK * pair_width)
    pick_ids = jnp.concatenate([wanted, glob_ids.astype(jnp.int32)])
    pick_hot = pick_ids[:, None] == jnp.arange(piece_blocks, dtype=jnp.int32)[None, :]
    picked = jnp.einsum(
        "pc,hcx->hpx", pick_hot.astype(jnp.bfloat16), grouped, preferred_element_type=jnp.float32
    ).astype(jnp.bfloat16)
    picked = picked.reshape(head_count, block_count * rand_count + glob_count, BLOCK, pair_width)
    random_pairs = picked[:, : block_count * rand_count].reshape(
        head_count, block_count, rand_count, BLOCK, pair_width
    )
    global_pairs = picked[:, block_count * rand_count :]
    global_wide = jnp.broadcast_to(
        global_pairs[:, None], (head_count, block_count, glob_count, BLOCK, pair_width)
    )
    key_pairs = jnp.concatenate([window_pairs, random_pairs, global_wide], axis=2)
    key_part = key_pairs[..., :head_width]
    value_part = key_pairs[..., head_width:]
    key_valid = jnp.concatenate(
        [window_ok, jnp.ones((block_count, rand_count + glob_count), dtype=bool)], axis=1
    )
    query_blocks = queries.reshape(head_count, block_count, BLOCK, head_width)
    cotan_blocks = grad_out.reshape(head_count, block_count, BLOCK, head_width)
    scores = (
        jnp.einsum("hiqd,hiskd->hiqsk", query_blocks, key_part, preferred_element_type=jnp.float32)
        * score_scale
    )
    scores = jnp.where(key_valid[None, :, None, :, None], scores, NEG_FILL)
    row_max = jnp.max(scores, axis=(3, 4), keepdims=True)
    expo_terms = jnp.exp(scores - row_max)
    weights = expo_terms / jnp.sum(expo_terms, axis=(3, 4), keepdims=True)
    weights_low = weights.astype(jnp.bfloat16)
    attended = jnp.einsum(
        "hiqsk,hiskd->hiqd", weights_low, value_part, preferred_element_type=jnp.float32
    )
    delta = jnp.sum(cotan_blocks.astype(jnp.float32) * attended, axis=3)
    grad_values = jnp.einsum(
        "hiqsk,hiqd->hiskd", weights_low, cotan_blocks, preferred_element_type=jnp.float32
    )
    grad_weights = jnp.einsum(
        "hiqd,hiskd->hiqsk", cotan_blocks, value_part, preferred_element_type=jnp.float32
    )
    grad_scores = (weights * (grad_weights - delta[:, :, :, None, None])).astype(jnp.bfloat16)
    grad_query = (
        jnp.einsum("hiqsk,hiskd->hiqd", grad_scores, key_part, preferred_element_type=jnp.float32)
        * score_scale
    )
    def key_terms(first, last):
        keys_now = jnp.einsum(
            "hiqsk,hiqd->hiskd",
            grad_scores[:, :, :, first:last],
            query_blocks,
            preferred_element_type=jnp.float32,
        )
        values_now = jnp.einsum(
            "hiqsk,hiqd->hiskd",
            weights_low[:, :, :, first:last],
            cotan_blocks,
            preferred_element_type=jnp.float32,
        )
        return jnp.concatenate([keys_now * score_scale, values_now], axis=4)

    random_terms = key_terms(3, 3 + rand_count).astype(jnp.bfloat16)
    random_terms = random_terms.reshape(head_count, block_count * rand_count, BLOCK * pair_width)
    slot_ids = jnp.arange(seq_count * slot_count, dtype=jnp.int32)
    send_hot = slot_ids[:, None] == return_at[None, :]
    outgoing_grads = jnp.einsum(
        "ti,hix->htx", send_hot.astype(jnp.bfloat16), random_terms, preferred_element_type=jnp.float32
    ).astype(jnp.bfloat16)
    outgoing_grads = outgoing_grads.reshape(head_count, seq_count, slot_count, BLOCK, pair_width)
    returned = lax.all_to_all(outgoing_grads, "seq", split_axis=1, concat_axis=1, tiled=True)
    window_terms = key_terms(0, 3)
    global_full = key_terms(3 + rand_count, 3 + rand_count + glob_count)
    wide_grad = jnp.pad(window_terms[:, :, 0], ((0, 0), (0, 2), (0, 0), (0, 0)))
    for offset in range(1, 3):
        wide_grad = wide_grad + jnp.pad(
            window_terms[:, :, offset], ((0, 0), (offset, 2 - offset), (0, 0), (0, 0))
        )
    edge_out = jnp.concatenate([wide_grad[:, 0], wide_grad[:, block_count + 1]], axis=1).astype(
        jnp.bfloat16
    )
    edge_out = edge_out.reshape(head_count, 2, BLOCK, pair_width)
    global_terms = jnp.sum(global_full, axis=1).astype(jnp.bfloat16)
    shared_out = jnp.concatenate([edge_out, global_terms], axis=1)
    shared_in = lax.all_gather(shared_out, "seq", axis=0)
    left_in = lax.dynamic_index_in_dim(shared_in, jnp.maximum(seq_place - 1, 0), 0, keepdims=False)
    right_in = lax.dynamic_index_in_dim(
        shared_in, jnp.minimum(seq_place + 1, seq_count - 1), 0, keepdims=False
    )
    from_left = jnp.where(seq_place > 0, left_in[:, 1].astype(jnp.float32), 0.0)
    from_right = jnp.where(seq_place < seq_count - 1, right_in[:, 0].astype(jnp.float32), 0.0)
    accum = wide_grad[:, 1 : block_count + 1]
    accum = accum.at[:, 0].add(from_left)
    accum = accum.at[:, block_count - 1].add(from_right)
    returned = returned.reshape(head_count, seq_count * slot_count, BLOCK * pair_width)
    block_hot = (
        send_block.reshape(-1)[:, None] == jnp.arange(block_count, dtype=jnp.int32)[None, :]
    ) & send_used.reshape(-1)[:, None]
    gathered = jnp.einsum(
        "cb,ecx->ebx", block_hot.astype(jnp.bfloat16), returned, preferred_element_type=jnp.float32
    )
    accum = accum + gathered.reshape(head_count, block_count, BLOCK, pair_width)
    global_sums = jnp.sum(shared_in[:, :, 2:].astype(jnp.float32), axis=0)
    at_first = (seq_place == 0).astype(jnp.float32)
    accum = accum.at[:, glob_ids].add(global_sums * at_first)
    grad_q = grad_query.reshape(head_count, row_count, head_width).astype(jnp.bfloat16)
    grad_k = accum[..., :head_width].reshape(head_count, row_count, head_width).astype(jnp.bfloat16)
    grad_v = accum[..., head_width:].reshape(head_count, row_count, head_width).astype(jnp.bfloat16)
    return (grad_q, grad_k, grad_v)


def solution(mesh):
    return jax.shard_map(
        local,
        mesh=mesh,
        in_specs=(
            P("head", "seq", None),
            P("head", "seq", None),
            P("head", "seq", None),
            P("head", "seq", None),
            P(),
            P(),
            P(),
        ),
        out_specs=(P("head", "seq", None), P("head", "seq", None), P("head", "seq", None)),
        check_vma=False,
    )
```

```python
import math

import jax
import jax.numpy as jnp
from jax import lax
from jax.sharding import PartitionSpec as P

BLOCK = 64


NEG_FILL = -1e30


def local(queries, keys, values, grad_out, rand_owner, rand_slot, glob_ids):
    head_count, row_count, head_width = queries.shape
    block_count = row_count // BLOCK
    rand_count = rand_owner.shape[1]
    glob_count = glob_ids.shape[0]
    seq_count = lax.axis_size("seq")
    seq_place = lax.axis_index("seq")
    slot_count = min(
        block_count, max(2, (2 * block_count * rand_count + seq_count - 1) // seq_count)
    )
    pair_width = 2 * head_width
    score_scale = 1.0 / math.sqrt(head_width)
    paired = jnp.concatenate([keys, values], axis=2)
    paired_blocks = paired.reshape(head_count, block_count, BLOCK, pair_width)
    piece_rows = lax.all_gather(paired, "seq", axis=1, tiled=True)
    row_start = seq_place * row_count
    edge_before = lax.dynamic_slice_in_dim(piece_rows, row_start - BLOCK, BLOCK, axis=1)
    edge_after = lax.dynamic_slice_in_dim(piece_rows, row_start + row_count, BLOCK, axis=1)
    widened = jnp.concatenate([edge_before, paired, edge_after], axis=1)
    widened = widened.reshape(head_count, block_count + 2, BLOCK, pair_width)
    window_pairs = jnp.stack(
        [widened[:, offset : offset + block_count] for offset in range(3)], axis=2
    )
    global_block = seq_place * block_count + jnp.arange(block_count, dtype=jnp.int32)
    window_ids = global_block[:, None] + jnp.arange(-1, 2, dtype=jnp.int32)[None, :]
    window_ok = (window_ids >= 0) & (window_ids < seq_count * block_count)
    owners_all = rand_owner.reshape(seq_count, block_count * rand_count)
    slots_all = rand_slot.reshape(seq_count, block_count * rand_count)
    owner_hot = (
        owners_all[:, :, None] == jnp.arange(seq_count, dtype=jnp.int32)[None, None, :]
    ).astype(jnp.int32)
    before = jnp.cumsum(owner_hot, axis=1) - owner_hot
    position = jnp.sum(before * owner_hot, axis=2)
    to_here = owners_all == seq_place
    slot_hot = (
        position[:, :, None] == jnp.arange(slot_count, dtype=jnp.int32)[None, None, :]
    ) & to_here[:, :, None]
    send_block = jnp.sum(slot_hot.astype(jnp.int32) * slots_all[:, :, None], axis=1)
    send_used = jnp.any(slot_hot, axis=1)
    my_owner = lax.dynamic_index_in_dim(owners_all, seq_place, 0, keepdims=False)
    my_slot = lax.dynamic_index_in_dim(slots_all, seq_place, 0, keepdims=False)
    my_position = lax.dynamic_index_in_dim(position, seq_place, 0, keepdims=False)
    return_at = my_owner * slot_count + my_position
    wanted = my_owner * block_count + my_slot
    piece_blocks = piece_rows.shape[1] // BLOCK
    grouped = piece_rows.reshape(head_count, piece_blocks, BLOCK, pair_width)
    pick_ids = jnp.concatenate([wanted, glob_ids.astype(jnp.int32)])
    picked = jnp.take(grouped, jnp.clip(pick_ids, 0, piece_blocks - 1), axis=1)
    random_pairs = picked[:, : block_count * rand_count].reshape(
        head_count, block_count, rand_count, BLOCK, pair_width
    )
    global_pairs = picked[:, block_count * rand_count :]
    global_wide = jnp.broadcast_to(
        global_pairs[:, None], (head_count, block_count, glob_count, BLOCK, pair_width)
    )
    key_pairs = jnp.concatenate([window_pairs, random_pairs, global_wide], axis=2)
    key_part = key_pairs[..., :head_width]
    value_part = key_pairs[..., head_width:]
    key_valid = jnp.concatenate(
        [window_ok, jnp.ones((block_count, rand_count + glob_count), dtype=bool)], axis=1
    )
    query_blocks = queries.reshape(head_count, block_count, BLOCK, head_width)
    cotan_blocks = grad_out.reshape(head_count, block_count, BLOCK, head_width)
    scores = (
        jnp.einsum("hiqd,hiskd->hiqsk", query_blocks, key_part, preferred_element_type=jnp.float32)
        * score_scale
    )
    scores = jnp.where(key_valid[None, :, None, :, None], scores, NEG_FILL)
    row_max = jnp.max(scores, axis=(3, 4), keepdims=True)
    expo_terms = jnp.exp(scores - row_max)
    weights = expo_terms / jnp.sum(expo_terms, axis=(3, 4), keepdims=True)
    weights_low = weights.astype(jnp.bfloat16)
    attended = jnp.einsum(
        "hiqsk,hiskd->hiqd", weights_low, value_part, preferred_element_type=jnp.float32
    )
    delta = jnp.sum(cotan_blocks.astype(jnp.float32) * attended, axis=3)
    grad_values = jnp.einsum(
        "hiqsk,hiqd->hiskd", weights_low, cotan_blocks, preferred_element_type=jnp.float32
    )
    grad_weights = jnp.einsum(
        "hiqd,hiskd->hiqsk", cotan_blocks, value_part, preferred_element_type=jnp.float32
    )
    grad_scores = (weights * (grad_weights - delta[:, :, :, None, None])).astype(jnp.bfloat16)
    grad_query = (
        jnp.einsum("hiqsk,hiskd->hiqd", grad_scores, key_part, preferred_element_type=jnp.float32)
        * score_scale
    )
    def key_terms(first, last):
        keys_now = jnp.einsum(
            "hiqsk,hiqd->hiskd",
            grad_scores[:, :, :, first:last],
            query_blocks,
            preferred_element_type=jnp.float32,
        )
        values_now = jnp.einsum(
            "hiqsk,hiqd->hiskd",
            weights_low[:, :, :, first:last],
            cotan_blocks,
            preferred_element_type=jnp.float32,
        )
        return jnp.concatenate([keys_now * score_scale, values_now], axis=4)

    random_terms = key_terms(3, 3 + rand_count).astype(jnp.bfloat16)
    random_terms = random_terms.reshape(head_count, block_count * rand_count, BLOCK * pair_width)
    slot_ids = jnp.arange(seq_count * slot_count, dtype=jnp.int32)
    send_hot = slot_ids[:, None] == return_at[None, :]
    outgoing_grads = jnp.einsum(
        "ti,hix->htx", send_hot.astype(jnp.bfloat16), random_terms, preferred_element_type=jnp.float32
    ).astype(jnp.bfloat16)
    outgoing_grads = outgoing_grads.reshape(head_count, seq_count, slot_count, BLOCK, pair_width)
    returned = lax.all_to_all(outgoing_grads, "seq", split_axis=1, concat_axis=1, tiled=True)
    window_terms = key_terms(0, 3)
    global_full = key_terms(3 + rand_count, 3 + rand_count + glob_count)
    wide_grad = jnp.pad(window_terms[:, :, 0], ((0, 0), (0, 2), (0, 0), (0, 0)))
    for offset in range(1, 3):
        wide_grad = wide_grad + jnp.pad(
            window_terms[:, :, offset], ((0, 0), (offset, 2 - offset), (0, 0), (0, 0))
        )
    edge_out = jnp.concatenate([wide_grad[:, 0], wide_grad[:, block_count + 1]], axis=1).astype(
        jnp.bfloat16
    )
    rightward = [(i, i + 1) for i in range(seq_count - 1)]
    leftward = [(i + 1, i) for i in range(seq_count - 1)]
    from_left = lax.ppermute(edge_out[:, BLOCK:], "seq", rightward).astype(jnp.float32)
    from_right = lax.ppermute(edge_out[:, :BLOCK], "seq", leftward).astype(jnp.float32)
    global_terms = jnp.sum(global_full, axis=1).astype(jnp.bfloat16)
    global_parts = lax.all_gather(global_terms, "seq", axis=0)
    accum = wide_grad[:, 1 : block_count + 1]
    accum = accum.at[:, 0].add(from_left)
    accum = accum.at[:, block_count - 1].add(from_right)
    returned = returned.reshape(head_count, seq_count * slot_count, BLOCK * pair_width)
    block_hot = (
        send_block.reshape(-1)[:, None] == jnp.arange(block_count, dtype=jnp.int32)[None, :]
    ) & send_used.reshape(-1)[:, None]
    gathered = jnp.einsum(
        "cb,ecx->ebx", block_hot.astype(jnp.bfloat16), returned, preferred_element_type=jnp.float32
    )
    accum = accum + gathered.reshape(head_count, block_count, BLOCK, pair_width)
    global_sums = jnp.sum(global_parts.astype(jnp.float32), axis=0)
    at_first = (seq_place == 0).astype(jnp.float32)
    accum = accum.at[:, glob_ids].add(global_sums * at_first)
    grad_q = grad_query.reshape(head_count, row_count, head_width).astype(jnp.bfloat16)
    grad_k = accum[..., :head_width].reshape(head_count, row_count, head_width).astype(jnp.bfloat16)
    grad_v = accum[..., head_width:].reshape(head_count, row_count, head_width).astype(jnp.bfloat16)
    return (grad_q, grad_k, grad_v)


def solution(mesh):
    return jax.shard_map(
        local,
        mesh=mesh,
        in_specs=(
            P("head", "seq", None),
            P("head", "seq", None),
            P("head", "seq", None),
            P("head", "seq", None),
            P(),
            P(),
            P(),
        ),
        out_specs=(P("head", "seq", None), P("head", "seq", None), P("head", "seq", None)),
        check_vma=False,
    )
```

```python
import math

import jax
import jax.numpy as jnp
from jax import lax
from jax.sharding import Mesh, PartitionSpec as P

BLOCK = 64


NEG_FILL = -1e30
SEQ = ("sz", "sc")


def local(queries, keys, values, grad_out, rand_owner, rand_slot, glob_ids):
    head_count, row_count, head_width = queries.shape
    block_count = row_count // BLOCK
    rand_count = rand_owner.shape[1]
    glob_count = glob_ids.shape[0]
    core_count = lax.axis_size("sc")
    core_place = lax.axis_index("sc")
    seq_count = lax.axis_size("sz") * core_count
    seq_place = lax.axis_index("sz") * core_count + core_place
    slot_count = min(
        block_count, max(2, (2 * block_count * rand_count + seq_count - 1) // seq_count)
    )
    pair_width = 2 * head_width
    score_scale = 1.0 / math.sqrt(head_width)
    paired = jnp.concatenate([keys, values], axis=2)
    paired_blocks = paired.reshape(head_count, block_count, BLOCK, pair_width)
    owners_all = rand_owner.reshape(seq_count, block_count * rand_count)
    slots_all = rand_slot.reshape(seq_count, block_count * rand_count)
    total_blocks = seq_count * block_count

    def pick_list(place):
        owner_now = lax.dynamic_index_in_dim(owners_all, place, 0, keepdims=False)
        slot_now = lax.dynamic_index_in_dim(slots_all, place, 0, keepdims=False)
        edge_ids = place * block_count + jnp.array([-1, block_count], jnp.int32)
        ids = jnp.concatenate([owner_now * block_count + slot_now, glob_ids.astype(jnp.int32), edge_ids])
        return jnp.clip(ids, 0, total_blocks - 1)

    def core_of(ids):
        return (ids // block_count) % core_count

    def row_of(ids):
        return (ids // block_count // core_count) * block_count + ids % block_count

    mine_ids = pick_list(seq_place)
    sibling_ids = pick_list(seq_place - core_place + (1 - core_place))
    core_rows = lax.all_gather(paired_blocks, "sz", axis=1, tiled=True)
    for_me = jnp.take(core_rows, row_of(mine_ids), axis=1)
    for_sibling = jnp.take(core_rows, row_of(sibling_ids), axis=1)
    from_sibling = lax.ppermute(for_sibling, "sc", [(0, 1), (1, 0)])
    picked = jnp.where(
        (core_of(mine_ids) == core_place)[None, :, None, None], for_me, from_sibling
    )
    pick_count = block_count * rand_count + glob_count
    widened = jnp.concatenate(
        [picked[:, pick_count : pick_count + 1], paired_blocks, picked[:, pick_count + 1 :]], axis=1
    )
    window_pairs = jnp.stack(
        [widened[:, offset : offset + block_count] for offset in range(3)], axis=2
    )
    global_block = seq_place * block_count + jnp.arange(block_count, dtype=jnp.int32)
    window_ids = global_block[:, None] + jnp.arange(-1, 2, dtype=jnp.int32)[None, :]
    window_ok = (window_ids >= 0) & (window_ids < seq_count * block_count)
    owner_hot = (
        owners_all[:, :, None] == jnp.arange(seq_count, dtype=jnp.int32)[None, None, :]
    ).astype(jnp.int32)
    before = jnp.cumsum(owner_hot, axis=1) - owner_hot
    position = jnp.sum(before * owner_hot, axis=2)
    to_here = owners_all == seq_place
    slot_hot = (
        position[:, :, None] == jnp.arange(slot_count, dtype=jnp.int32)[None, None, :]
    ) & to_here[:, :, None]
    send_block = jnp.sum(slot_hot.astype(jnp.int32) * slots_all[:, :, None], axis=1)
    send_used = jnp.any(slot_hot, axis=1)
    my_owner = lax.dynamic_index_in_dim(owners_all, seq_place, 0, keepdims=False)
    my_slot = lax.dynamic_index_in_dim(slots_all, seq_place, 0, keepdims=False)
    my_position = lax.dynamic_index_in_dim(position, seq_place, 0, keepdims=False)
    return_at = my_owner * slot_count + my_position
    wanted = my_owner * block_count + my_slot
    random_pairs = picked[:, : block_count * rand_count].reshape(
        head_count, block_count, rand_count, BLOCK, pair_width
    )
    global_pairs = picked[:, block_count * rand_count : pick_count]
    global_wide = jnp.broadcast_to(
        global_pairs[:, None], (head_count, block_count, glob_count, BLOCK, pair_width)
    )
    key_pairs = jnp.concatenate([window_pairs, random_pairs, global_wide], axis=2)
    key_part = key_pairs[..., :head_width]
    value_part = key_pairs[..., head_width:]
    key_valid = jnp.concatenate(
        [window_ok, jnp.ones((block_count, rand_count + glob_count), dtype=bool)], axis=1
    )
    query_blocks = queries.reshape(head_count, block_count, BLOCK, head_width)
    cotan_blocks = grad_out.reshape(head_count, block_count, BLOCK, head_width)
    scores = (
        jnp.einsum("hiqd,hiskd->hiqsk", query_blocks, key_part, preferred_element_type=jnp.float32)
        * score_scale
    )
    scores = jnp.where(key_valid[None, :, None, :, None], scores, NEG_FILL)
    row_max = jnp.max(scores, axis=(3, 4), keepdims=True)
    expo_terms = jnp.exp(scores - row_max)
    weights = expo_terms / jnp.sum(expo_terms, axis=(3, 4), keepdims=True)
    weights_low = weights.astype(jnp.bfloat16)
    attended = jnp.einsum(
        "hiqsk,hiskd->hiqd", weights_low, value_part, preferred_element_type=jnp.float32
    )
    delta = jnp.sum(cotan_blocks.astype(jnp.float32) * attended, axis=3)
    grad_values = jnp.einsum(
        "hiqsk,hiqd->hiskd", weights_low, cotan_blocks, preferred_element_type=jnp.float32
    )
    grad_weights = jnp.einsum(
        "hiqd,hiskd->hiqsk", cotan_blocks, value_part, preferred_element_type=jnp.float32
    )
    grad_scores = (weights * (grad_weights - delta[:, :, :, None, None])).astype(jnp.bfloat16)
    grad_query = (
        jnp.einsum("hiqsk,hiskd->hiqd", grad_scores, key_part, preferred_element_type=jnp.float32)
        * score_scale
    )
    def key_terms(first, last):
        keys_now = jnp.einsum(
            "hiqsk,hiqd->hiskd",
            grad_scores[:, :, :, first:last],
            query_blocks,
            preferred_element_type=jnp.float32,
        )
        values_now = jnp.einsum(
            "hiqsk,hiqd->hiskd",
            weights_low[:, :, :, first:last],
            cotan_blocks,
            preferred_element_type=jnp.float32,
        )
        return jnp.concatenate([keys_now * score_scale, values_now], axis=4)

    random_terms = key_terms(3, 3 + rand_count).astype(jnp.bfloat16)
    random_terms = random_terms.reshape(head_count, block_count * rand_count, BLOCK * pair_width)
    slot_ids = jnp.arange(seq_count * slot_count, dtype=jnp.int32)
    send_hot = slot_ids[:, None] == return_at[None, :]
    outgoing_grads = jnp.einsum(
        "ti,hix->htx", send_hot.astype(jnp.bfloat16), random_terms, preferred_element_type=jnp.float32
    ).astype(jnp.bfloat16)
    outgoing_grads = outgoing_grads.reshape(head_count, seq_count, slot_count, BLOCK, pair_width)
    returned = lax.all_to_all(outgoing_grads, SEQ, split_axis=1, concat_axis=1, tiled=True)
    window_terms = key_terms(0, 3)
    global_full = key_terms(3 + rand_count, 3 + rand_count + glob_count)
    wide_grad = jnp.pad(window_terms[:, :, 0], ((0, 0), (0, 2), (0, 0), (0, 0)))
    for offset in range(1, 3):
        wide_grad = wide_grad + jnp.pad(
            window_terms[:, :, offset], ((0, 0), (offset, 2 - offset), (0, 0), (0, 0))
        )
    edge_out = jnp.concatenate([wide_grad[:, 0], wide_grad[:, block_count + 1]], axis=1).astype(
        jnp.bfloat16
    )
    rightward = [(i, i + 1) for i in range(seq_count - 1)]
    leftward = [(i + 1, i) for i in range(seq_count - 1)]
    from_left = lax.ppermute(edge_out[:, BLOCK:], SEQ, rightward).astype(jnp.float32)
    from_right = lax.ppermute(edge_out[:, :BLOCK], SEQ, leftward).astype(jnp.float32)
    global_terms = jnp.sum(global_full, axis=1).astype(jnp.bfloat16)
    global_parts = lax.all_gather(global_terms, SEQ, axis=0)
    accum = wide_grad[:, 1 : block_count + 1]
    accum = accum.at[:, 0].add(from_left)
    accum = accum.at[:, block_count - 1].add(from_right)
    returned = returned.reshape(head_count, seq_count * slot_count, BLOCK * pair_width)
    block_hot = (
        send_block.reshape(-1)[:, None] == jnp.arange(block_count, dtype=jnp.int32)[None, :]
    ) & send_used.reshape(-1)[:, None]
    gathered = jnp.einsum(
        "cb,ecx->ebx", block_hot.astype(jnp.bfloat16), returned, preferred_element_type=jnp.float32
    )
    accum = accum + gathered.reshape(head_count, block_count, BLOCK, pair_width)
    global_sums = jnp.sum(global_parts.astype(jnp.float32), axis=0)
    at_first = (seq_place == 0).astype(jnp.float32)
    accum = accum.at[:, glob_ids].add(global_sums * at_first)
    grad_q = grad_query.reshape(head_count, row_count, head_width).astype(jnp.bfloat16)
    grad_k = accum[..., :head_width].reshape(head_count, row_count, head_width).astype(jnp.bfloat16)
    grad_v = accum[..., head_width:].reshape(head_count, row_count, head_width).astype(jnp.bfloat16)
    return (grad_q, grad_k, grad_v)


def solution(mesh):
    seq_size = mesh.shape["seq"]
    core_size = 2
    devices = mesh.devices.reshape(seq_size // core_size, core_size, mesh.shape["head"])
    split_mesh = Mesh(devices, ("sz", "sc", "head"))
    rows = P("head", SEQ, None)
    return jax.shard_map(
        local,
        mesh=split_mesh,
        in_specs=(rows, rows, rows, rows, P(), P(), P()),
        out_specs=(rows, rows, rows),
        check_vma=False,
    )
```

```python
import math

import jax
import jax.numpy as jnp
from jax import lax
from jax.sharding import Mesh, PartitionSpec as P

BLOCK = 64


NEG_FILL = -1e30
SEQ = ("sz", "sc")


def local(queries, keys, values, grad_out, rand_owner, rand_slot, glob_ids):
    head_count, row_count, head_width = queries.shape
    block_count = row_count // BLOCK
    rand_count = rand_owner.shape[1]
    glob_count = glob_ids.shape[0]
    core_count = lax.axis_size("sc")
    core_place = lax.axis_index("sc")
    seq_count = lax.axis_size("sz") * core_count
    seq_place = lax.axis_index("sz") * core_count + core_place
    slot_count = min(
        block_count, max(2, (2 * block_count * rand_count + seq_count - 1) // seq_count)
    )
    pair_width = 2 * head_width
    score_scale = 1.0 / math.sqrt(head_width)
    paired = jnp.concatenate([keys, values], axis=2)
    paired_blocks = paired.reshape(head_count, block_count, BLOCK, pair_width)
    owners_all = rand_owner.reshape(seq_count, block_count * rand_count)
    slots_all = rand_slot.reshape(seq_count, block_count * rand_count)
    total_blocks = seq_count * block_count

    def pick_list(place):
        owner_now = lax.dynamic_index_in_dim(owners_all, place, 0, keepdims=False)
        slot_now = lax.dynamic_index_in_dim(slots_all, place, 0, keepdims=False)
        edge_ids = place * block_count + jnp.array([-1, block_count], jnp.int32)
        ids = jnp.concatenate([owner_now * block_count + slot_now, glob_ids.astype(jnp.int32), edge_ids])
        return jnp.clip(ids, 0, total_blocks - 1)

    def row_of(ids):
        seq_of = ids // block_count
        order_of = (seq_of % core_count) * (seq_count // core_count) + seq_of // core_count
        return order_of * block_count + ids % block_count

    mine_ids = pick_list(seq_place)
    all_rows = lax.all_gather(paired_blocks, ("sc", "sz"), axis=1, tiled=True)
    picked = jnp.take(all_rows, row_of(mine_ids), axis=1)
    pick_count = block_count * rand_count + glob_count
    widened = jnp.concatenate(
        [picked[:, pick_count : pick_count + 1], paired_blocks, picked[:, pick_count + 1 :]], axis=1
    )
    window_pairs = jnp.stack(
        [widened[:, offset : offset + block_count] for offset in range(3)], axis=2
    )
    global_block = seq_place * block_count + jnp.arange(block_count, dtype=jnp.int32)
    window_ids = global_block[:, None] + jnp.arange(-1, 2, dtype=jnp.int32)[None, :]
    window_ok = (window_ids >= 0) & (window_ids < seq_count * block_count)
    owner_hot = (
        owners_all[:, :, None] == jnp.arange(seq_count, dtype=jnp.int32)[None, None, :]
    ).astype(jnp.int32)
    before = jnp.cumsum(owner_hot, axis=1) - owner_hot
    position = jnp.sum(before * owner_hot, axis=2)
    to_here = owners_all == seq_place
    slot_hot = (
        position[:, :, None] == jnp.arange(slot_count, dtype=jnp.int32)[None, None, :]
    ) & to_here[:, :, None]
    send_block = jnp.sum(slot_hot.astype(jnp.int32) * slots_all[:, :, None], axis=1)
    send_used = jnp.any(slot_hot, axis=1)
    my_owner = lax.dynamic_index_in_dim(owners_all, seq_place, 0, keepdims=False)
    my_slot = lax.dynamic_index_in_dim(slots_all, seq_place, 0, keepdims=False)
    my_position = lax.dynamic_index_in_dim(position, seq_place, 0, keepdims=False)
    return_at = my_owner * slot_count + my_position
    wanted = my_owner * block_count + my_slot
    random_pairs = picked[:, : block_count * rand_count].reshape(
        head_count, block_count, rand_count, BLOCK, pair_width
    )
    global_pairs = picked[:, block_count * rand_count : pick_count]
    global_wide = jnp.broadcast_to(
        global_pairs[:, None], (head_count, block_count, glob_count, BLOCK, pair_width)
    )
    key_pairs = jnp.concatenate([window_pairs, random_pairs, global_wide], axis=2)
    key_part = key_pairs[..., :head_width]
    value_part = key_pairs[..., head_width:]
    key_valid = jnp.concatenate(
        [window_ok, jnp.ones((block_count, rand_count + glob_count), dtype=bool)], axis=1
    )
    query_blocks = queries.reshape(head_count, block_count, BLOCK, head_width)
    cotan_blocks = grad_out.reshape(head_count, block_count, BLOCK, head_width)
    scores = (
        jnp.einsum("hiqd,hiskd->hiqsk", query_blocks, key_part, preferred_element_type=jnp.float32)
        * score_scale
    )
    scores = jnp.where(key_valid[None, :, None, :, None], scores, NEG_FILL)
    row_max = jnp.max(scores, axis=(3, 4), keepdims=True)
    expo_terms = jnp.exp(scores - row_max)
    weights = expo_terms / jnp.sum(expo_terms, axis=(3, 4), keepdims=True)
    weights_low = weights.astype(jnp.bfloat16)
    attended = jnp.einsum(
        "hiqsk,hiskd->hiqd", weights_low, value_part, preferred_element_type=jnp.float32
    )
    delta = jnp.sum(cotan_blocks.astype(jnp.float32) * attended, axis=3)
    grad_values = jnp.einsum(
        "hiqsk,hiqd->hiskd", weights_low, cotan_blocks, preferred_element_type=jnp.float32
    )
    grad_weights = jnp.einsum(
        "hiqd,hiskd->hiqsk", cotan_blocks, value_part, preferred_element_type=jnp.float32
    )
    grad_scores = (weights * (grad_weights - delta[:, :, :, None, None])).astype(jnp.bfloat16)
    grad_query = (
        jnp.einsum("hiqsk,hiskd->hiqd", grad_scores, key_part, preferred_element_type=jnp.float32)
        * score_scale
    )
    def key_terms(first, last):
        keys_now = jnp.einsum(
            "hiqsk,hiqd->hiskd",
            grad_scores[:, :, :, first:last],
            query_blocks,
            preferred_element_type=jnp.float32,
        )
        values_now = jnp.einsum(
            "hiqsk,hiqd->hiskd",
            weights_low[:, :, :, first:last],
            cotan_blocks,
            preferred_element_type=jnp.float32,
        )
        return jnp.concatenate([keys_now * score_scale, values_now], axis=4)

    random_terms = key_terms(3, 3 + rand_count).astype(jnp.bfloat16)
    random_terms = random_terms.reshape(head_count, block_count * rand_count, BLOCK * pair_width)
    slot_ids = jnp.arange(seq_count * slot_count, dtype=jnp.int32)
    send_hot = slot_ids[:, None] == return_at[None, :]
    outgoing_grads = jnp.einsum(
        "ti,hix->htx", send_hot.astype(jnp.bfloat16), random_terms, preferred_element_type=jnp.float32
    ).astype(jnp.bfloat16)
    outgoing_grads = outgoing_grads.reshape(head_count, seq_count, slot_count, BLOCK, pair_width)
    returned = lax.all_to_all(outgoing_grads, SEQ, split_axis=1, concat_axis=1, tiled=True)
    window_terms = key_terms(0, 3)
    global_full = key_terms(3 + rand_count, 3 + rand_count + glob_count)
    wide_grad = jnp.pad(window_terms[:, :, 0], ((0, 0), (0, 2), (0, 0), (0, 0)))
    for offset in range(1, 3):
        wide_grad = wide_grad + jnp.pad(
            window_terms[:, :, offset], ((0, 0), (offset, 2 - offset), (0, 0), (0, 0))
        )
    edge_out = jnp.concatenate([wide_grad[:, 0], wide_grad[:, block_count + 1]], axis=1).astype(
        jnp.bfloat16
    )
    rightward = [(i, i + 1) for i in range(seq_count - 1)]
    leftward = [(i + 1, i) for i in range(seq_count - 1)]
    from_left = lax.ppermute(edge_out[:, BLOCK:], SEQ, rightward).astype(jnp.float32)
    from_right = lax.ppermute(edge_out[:, :BLOCK], SEQ, leftward).astype(jnp.float32)
    global_terms = jnp.sum(global_full, axis=1).astype(jnp.bfloat16)
    global_parts = lax.all_gather(global_terms, SEQ, axis=0)
    accum = wide_grad[:, 1 : block_count + 1]
    accum = accum.at[:, 0].add(from_left)
    accum = accum.at[:, block_count - 1].add(from_right)
    returned = returned.reshape(head_count, seq_count * slot_count, BLOCK * pair_width)
    block_hot = (
        send_block.reshape(-1)[:, None] == jnp.arange(block_count, dtype=jnp.int32)[None, :]
    ) & send_used.reshape(-1)[:, None]
    gathered = jnp.einsum(
        "cb,ecx->ebx", block_hot.astype(jnp.bfloat16), returned, preferred_element_type=jnp.float32
    )
    accum = accum + gathered.reshape(head_count, block_count, BLOCK, pair_width)
    global_sums = jnp.sum(global_parts.astype(jnp.float32), axis=0)
    at_first = (seq_place == 0).astype(jnp.float32)
    accum = accum.at[:, glob_ids].add(global_sums * at_first)
    grad_q = grad_query.reshape(head_count, row_count, head_width).astype(jnp.bfloat16)
    grad_k = accum[..., :head_width].reshape(head_count, row_count, head_width).astype(jnp.bfloat16)
    grad_v = accum[..., head_width:].reshape(head_count, row_count, head_width).astype(jnp.bfloat16)
    return (grad_q, grad_k, grad_v)


def solution(mesh):
    seq_size = mesh.shape["seq"]
    core_size = 2
    devices = mesh.devices.reshape(seq_size // core_size, core_size, mesh.shape["head"])
    split_mesh = Mesh(devices, ("sz", "sc", "head"))
    rows = P("head", SEQ, None)
    return jax.shard_map(
        local,
        mesh=split_mesh,
        in_specs=(rows, rows, rows, rows, P(), P(), P()),
        out_specs=(rows, rows, rows),
        check_vma=False,
    )
```

```python
import math

import jax
import jax.numpy as jnp
from jax import lax
from jax.sharding import PartitionSpec as P

BLOCK = 64


NEG_FILL = -1e30


def local(queries, keys, values, grad_out, rand_owner, rand_slot, glob_ids):
    head_count, row_count, head_width = queries.shape
    block_count = row_count // BLOCK
    rand_count = rand_owner.shape[1]
    glob_count = glob_ids.shape[0]
    seq_count = lax.axis_size("seq")
    seq_place = lax.axis_index("seq")
    slot_count = min(
        block_count, max(2, (2 * block_count * rand_count + seq_count - 1) // seq_count)
    )
    pair_width = 2 * head_width
    score_scale = 1.0 / math.sqrt(head_width)
    paired = jnp.concatenate([keys, values], axis=2)
    paired_blocks = paired.reshape(head_count, block_count, BLOCK, pair_width)
    piece_rows = lax.all_gather(paired, "seq", axis=1, tiled=True)
    row_start = seq_place * row_count
    edge_before = lax.dynamic_slice_in_dim(piece_rows, row_start - BLOCK, BLOCK, axis=1)
    edge_after = lax.dynamic_slice_in_dim(piece_rows, row_start + row_count, BLOCK, axis=1)
    widened = jnp.concatenate([edge_before, paired, edge_after], axis=1)
    widened = widened.reshape(head_count, block_count + 2, BLOCK, pair_width)
    window_pairs = jnp.stack(
        [widened[:, offset : offset + block_count] for offset in range(3)], axis=2
    )
    global_block = seq_place * block_count + jnp.arange(block_count, dtype=jnp.int32)
    window_ids = global_block[:, None] + jnp.arange(-1, 2, dtype=jnp.int32)[None, :]
    window_ok = (window_ids >= 0) & (window_ids < seq_count * block_count)
    owners_all = rand_owner.reshape(seq_count, block_count * rand_count)
    slots_all = rand_slot.reshape(seq_count, block_count * rand_count)
    owner_hot = (
        owners_all[:, :, None] == jnp.arange(seq_count, dtype=jnp.int32)[None, None, :]
    ).astype(jnp.int32)
    before = jnp.cumsum(owner_hot, axis=1) - owner_hot
    position = jnp.sum(before * owner_hot, axis=2)
    to_here = owners_all == seq_place
    slot_hot = (
        position[:, :, None] == jnp.arange(slot_count, dtype=jnp.int32)[None, None, :]
    ) & to_here[:, :, None]
    send_block = jnp.sum(slot_hot.astype(jnp.int32) * slots_all[:, :, None], axis=1)
    send_used = jnp.any(slot_hot, axis=1)
    my_owner = lax.dynamic_index_in_dim(owners_all, seq_place, 0, keepdims=False)
    my_slot = lax.dynamic_index_in_dim(slots_all, seq_place, 0, keepdims=False)
    my_position = lax.dynamic_index_in_dim(position, seq_place, 0, keepdims=False)
    return_at = my_owner * slot_count + my_position
    wanted = my_owner * block_count + my_slot
    piece_blocks = piece_rows.shape[1] // BLOCK
    grouped = piece_rows.reshape(head_count, piece_blocks, BLOCK, pair_width)
    pick_ids = jnp.concatenate([wanted, glob_ids.astype(jnp.int32)])
    pick_at = jnp.clip(pick_ids, 0, piece_blocks - 1)
    picked = jnp.concatenate(
        [
            lax.dynamic_slice_in_dim(grouped, pick_at[index], 1, axis=1)
            for index in range(pick_ids.shape[0])
        ],
        axis=1,
    )
    random_pairs = picked[:, : block_count * rand_count].reshape(
        head_count, block_count, rand_count, BLOCK, pair_width
    )
    global_pairs = picked[:, block_count * rand_count :]
    global_wide = jnp.broadcast_to(
        global_pairs[:, None], (head_count, block_count, glob_count, BLOCK, pair_width)
    )
    key_pairs = jnp.concatenate([window_pairs, random_pairs, global_wide], axis=2)
    key_part = key_pairs[..., :head_width]
    value_part = key_pairs[..., head_width:]
    key_valid = jnp.concatenate(
        [window_ok, jnp.ones((block_count, rand_count + glob_count), dtype=bool)], axis=1
    )
    query_blocks = queries.reshape(head_count, block_count, BLOCK, head_width)
    cotan_blocks = grad_out.reshape(head_count, block_count, BLOCK, head_width)
    scores = (
        jnp.einsum("hiqd,hiskd->hiqsk", query_blocks, key_part, preferred_element_type=jnp.float32)
        * score_scale
    )
    scores = jnp.where(key_valid[None, :, None, :, None], scores, NEG_FILL)
    row_max = jnp.max(scores, axis=(3, 4), keepdims=True)
    expo_terms = jnp.exp(scores - row_max)
    weights = expo_terms / jnp.sum(expo_terms, axis=(3, 4), keepdims=True)
    weights_low = weights.astype(jnp.bfloat16)
    attended = jnp.einsum(
        "hiqsk,hiskd->hiqd", weights_low, value_part, preferred_element_type=jnp.float32
    )
    delta = jnp.sum(cotan_blocks.astype(jnp.float32) * attended, axis=3)
    grad_values = jnp.einsum(
        "hiqsk,hiqd->hiskd", weights_low, cotan_blocks, preferred_element_type=jnp.float32
    )
    grad_weights = jnp.einsum(
        "hiqd,hiskd->hiqsk", cotan_blocks, value_part, preferred_element_type=jnp.float32
    )
    grad_scores = (weights * (grad_weights - delta[:, :, :, None, None])).astype(jnp.bfloat16)
    grad_query = (
        jnp.einsum("hiqsk,hiskd->hiqd", grad_scores, key_part, preferred_element_type=jnp.float32)
        * score_scale
    )
    def key_terms(first, last):
        keys_now = jnp.einsum(
            "hiqsk,hiqd->hiskd",
            grad_scores[:, :, :, first:last],
            query_blocks,
            preferred_element_type=jnp.float32,
        )
        values_now = jnp.einsum(
            "hiqsk,hiqd->hiskd",
            weights_low[:, :, :, first:last],
            cotan_blocks,
            preferred_element_type=jnp.float32,
        )
        return jnp.concatenate([keys_now * score_scale, values_now], axis=4)

    random_terms = key_terms(3, 3 + rand_count).astype(jnp.bfloat16)
    random_terms = random_terms.reshape(head_count, block_count * rand_count, BLOCK * pair_width)
    slot_ids = jnp.arange(seq_count * slot_count, dtype=jnp.int32)
    send_hot = slot_ids[:, None] == return_at[None, :]
    outgoing_grads = jnp.einsum(
        "ti,hix->htx", send_hot.astype(jnp.bfloat16), random_terms, preferred_element_type=jnp.float32
    ).astype(jnp.bfloat16)
    outgoing_grads = outgoing_grads.reshape(head_count, seq_count, slot_count, BLOCK, pair_width)
    returned = lax.all_to_all(outgoing_grads, "seq", split_axis=1, concat_axis=1, tiled=True)
    window_terms = key_terms(0, 3)
    global_full = key_terms(3 + rand_count, 3 + rand_count + glob_count)
    wide_grad = jnp.pad(window_terms[:, :, 0], ((0, 0), (0, 2), (0, 0), (0, 0)))
    for offset in range(1, 3):
        wide_grad = wide_grad + jnp.pad(
            window_terms[:, :, offset], ((0, 0), (offset, 2 - offset), (0, 0), (0, 0))
        )
    edge_out = jnp.concatenate([wide_grad[:, 0], wide_grad[:, block_count + 1]], axis=1).astype(
        jnp.bfloat16
    )
    rightward = [(i, i + 1) for i in range(seq_count - 1)]
    leftward = [(i + 1, i) for i in range(seq_count - 1)]
    from_left = lax.ppermute(edge_out[:, BLOCK:], "seq", rightward).astype(jnp.float32)
    from_right = lax.ppermute(edge_out[:, :BLOCK], "seq", leftward).astype(jnp.float32)
    global_terms = jnp.sum(global_full, axis=1).astype(jnp.bfloat16)
    global_parts = lax.all_gather(global_terms, "seq", axis=0)
    accum = wide_grad[:, 1 : block_count + 1]
    accum = accum.at[:, 0].add(from_left)
    accum = accum.at[:, block_count - 1].add(from_right)
    returned = returned.reshape(head_count, seq_count * slot_count, BLOCK * pair_width)
    block_hot = (
        send_block.reshape(-1)[:, None] == jnp.arange(block_count, dtype=jnp.int32)[None, :]
    ) & send_used.reshape(-1)[:, None]
    gathered = jnp.einsum(
        "cb,ecx->ebx", block_hot.astype(jnp.bfloat16), returned, preferred_element_type=jnp.float32
    )
    accum = accum + gathered.reshape(head_count, block_count, BLOCK, pair_width)
    global_sums = jnp.sum(global_parts.astype(jnp.float32), axis=0)
    at_first = (seq_place == 0).astype(jnp.float32)
    accum = accum.at[:, glob_ids].add(global_sums * at_first)
    grad_q = grad_query.reshape(head_count, row_count, head_width).astype(jnp.bfloat16)
    grad_k = accum[..., :head_width].reshape(head_count, row_count, head_width).astype(jnp.bfloat16)
    grad_v = accum[..., head_width:].reshape(head_count, row_count, head_width).astype(jnp.bfloat16)
    return (grad_q, grad_k, grad_v)


def solution(mesh):
    return jax.shard_map(
        local,
        mesh=mesh,
        in_specs=(
            P("head", "seq", None),
            P("head", "seq", None),
            P("head", "seq", None),
            P("head", "seq", None),
            P(),
            P(),
            P(),
        ),
        out_specs=(P("head", "seq", None), P("head", "seq", None), P("head", "seq", None)),
        check_vma=False,
    )
```

```python
import math

import jax
import jax.numpy as jnp
from jax import lax
from jax.sharding import Mesh, PartitionSpec as P

BLOCK = 64


NEG_FILL = -1e30
SEQ = ("sz", "sc")


def local(queries, keys, values, grad_out, rand_owner, rand_slot, glob_ids):
    head_count, row_count, head_width = queries.shape
    block_count = row_count // BLOCK
    rand_count = rand_owner.shape[1]
    glob_count = glob_ids.shape[0]
    core_count = lax.axis_size("sc")
    core_place = lax.axis_index("sc")
    seq_count = lax.axis_size("sz") * core_count
    seq_place = lax.axis_index("sz") * core_count + core_place
    slot_count = min(
        block_count, max(2, (2 * block_count * rand_count + seq_count - 1) // seq_count)
    )
    pair_width = 2 * head_width
    score_scale = 1.0 / math.sqrt(head_width)
    paired = jnp.concatenate([keys, values], axis=2)
    paired_blocks = paired.reshape(head_count, block_count, BLOCK, pair_width)
    owners_all = rand_owner.reshape(seq_count, block_count * rand_count)
    slots_all = rand_slot.reshape(seq_count, block_count * rand_count)
    total_blocks = seq_count * block_count

    def pick_list(place):
        owner_now = lax.dynamic_index_in_dim(owners_all, place, 0, keepdims=False)
        slot_now = lax.dynamic_index_in_dim(slots_all, place, 0, keepdims=False)
        edge_ids = place * block_count + jnp.array([-1, block_count], jnp.int32)
        ids = jnp.concatenate([owner_now * block_count + slot_now, glob_ids.astype(jnp.int32), edge_ids])
        return jnp.clip(ids, 0, total_blocks - 1)

    mine_ids = pick_list(seq_place)
    sibling_blocks = lax.ppermute(paired_blocks, "sc", [(0, 1), (1, 0)])
    chip_blocks = jnp.where(
        core_place == 0,
        jnp.concatenate([paired_blocks, sibling_blocks], axis=1),
        jnp.concatenate([sibling_blocks, paired_blocks], axis=1),
    )
    all_rows = lax.all_gather(chip_blocks, "sz", axis=1, tiled=True)
    picked = jnp.take(all_rows, mine_ids, axis=1)
    pick_count = block_count * rand_count + glob_count
    widened = jnp.concatenate(
        [picked[:, pick_count : pick_count + 1], paired_blocks, picked[:, pick_count + 1 :]], axis=1
    )
    window_pairs = jnp.stack(
        [widened[:, offset : offset + block_count] for offset in range(3)], axis=2
    )
    global_block = seq_place * block_count + jnp.arange(block_count, dtype=jnp.int32)
    window_ids = global_block[:, None] + jnp.arange(-1, 2, dtype=jnp.int32)[None, :]
    window_ok = (window_ids >= 0) & (window_ids < seq_count * block_count)
    owner_hot = (
        owners_all[:, :, None] == jnp.arange(seq_count, dtype=jnp.int32)[None, None, :]
    ).astype(jnp.int32)
    before = jnp.cumsum(owner_hot, axis=1) - owner_hot
    position = jnp.sum(before * owner_hot, axis=2)
    to_here = owners_all == seq_place
    slot_hot = (
        position[:, :, None] == jnp.arange(slot_count, dtype=jnp.int32)[None, None, :]
    ) & to_here[:, :, None]
    send_block = jnp.sum(slot_hot.astype(jnp.int32) * slots_all[:, :, None], axis=1)
    send_used = jnp.any(slot_hot, axis=1)
    my_owner = lax.dynamic_index_in_dim(owners_all, seq_place, 0, keepdims=False)
    my_slot = lax.dynamic_index_in_dim(slots_all, seq_place, 0, keepdims=False)
    my_position = lax.dynamic_index_in_dim(position, seq_place, 0, keepdims=False)
    return_at = my_owner * slot_count + my_position
    wanted = my_owner * block_count + my_slot
    random_pairs = picked[:, : block_count * rand_count].reshape(
        head_count, block_count, rand_count, BLOCK, pair_width
    )
    global_pairs = picked[:, block_count * rand_count : pick_count]
    global_wide = jnp.broadcast_to(
        global_pairs[:, None], (head_count, block_count, glob_count, BLOCK, pair_width)
    )
    key_pairs = jnp.concatenate([window_pairs, random_pairs, global_wide], axis=2)
    key_part = key_pairs[..., :head_width]
    value_part = key_pairs[..., head_width:]
    key_valid = jnp.concatenate(
        [window_ok, jnp.ones((block_count, rand_count + glob_count), dtype=bool)], axis=1
    )
    query_blocks = queries.reshape(head_count, block_count, BLOCK, head_width)
    cotan_blocks = grad_out.reshape(head_count, block_count, BLOCK, head_width)
    scores = (
        jnp.einsum("hiqd,hiskd->hiqsk", query_blocks, key_part, preferred_element_type=jnp.float32)
        * score_scale
    )
    scores = jnp.where(key_valid[None, :, None, :, None], scores, NEG_FILL)
    row_max = jnp.max(scores, axis=(3, 4), keepdims=True)
    expo_terms = jnp.exp(scores - row_max)
    weights = expo_terms / jnp.sum(expo_terms, axis=(3, 4), keepdims=True)
    weights_low = weights.astype(jnp.bfloat16)
    attended = jnp.einsum(
        "hiqsk,hiskd->hiqd", weights_low, value_part, preferred_element_type=jnp.float32
    )
    delta = jnp.sum(cotan_blocks.astype(jnp.float32) * attended, axis=3)
    grad_values = jnp.einsum(
        "hiqsk,hiqd->hiskd", weights_low, cotan_blocks, preferred_element_type=jnp.float32
    )
    grad_weights = jnp.einsum(
        "hiqd,hiskd->hiqsk", cotan_blocks, value_part, preferred_element_type=jnp.float32
    )
    grad_scores = (weights * (grad_weights - delta[:, :, :, None, None])).astype(jnp.bfloat16)
    grad_query = (
        jnp.einsum("hiqsk,hiskd->hiqd", grad_scores, key_part, preferred_element_type=jnp.float32)
        * score_scale
    )
    def key_terms(first, last):
        keys_now = jnp.einsum(
            "hiqsk,hiqd->hiskd",
            grad_scores[:, :, :, first:last],
            query_blocks,
            preferred_element_type=jnp.float32,
        )
        values_now = jnp.einsum(
            "hiqsk,hiqd->hiskd",
            weights_low[:, :, :, first:last],
            cotan_blocks,
            preferred_element_type=jnp.float32,
        )
        return jnp.concatenate([keys_now * score_scale, values_now], axis=4)

    random_terms = key_terms(3, 3 + rand_count).astype(jnp.bfloat16)
    random_terms = random_terms.reshape(head_count, block_count * rand_count, BLOCK * pair_width)
    slot_ids = jnp.arange(seq_count * slot_count, dtype=jnp.int32)
    send_hot = slot_ids[:, None] == return_at[None, :]
    outgoing_grads = jnp.einsum(
        "ti,hix->htx", send_hot.astype(jnp.bfloat16), random_terms, preferred_element_type=jnp.float32
    ).astype(jnp.bfloat16)
    outgoing_grads = outgoing_grads.reshape(head_count, seq_count, slot_count, BLOCK, pair_width)
    returned = lax.all_to_all(outgoing_grads, SEQ, split_axis=1, concat_axis=1, tiled=True)
    window_terms = key_terms(0, 3)
    global_full = key_terms(3 + rand_count, 3 + rand_count + glob_count)
    wide_grad = jnp.pad(window_terms[:, :, 0], ((0, 0), (0, 2), (0, 0), (0, 0)))
    for offset in range(1, 3):
        wide_grad = wide_grad + jnp.pad(
            window_terms[:, :, offset], ((0, 0), (offset, 2 - offset), (0, 0), (0, 0))
        )
    edge_out = jnp.concatenate([wide_grad[:, 0], wide_grad[:, block_count + 1]], axis=1).astype(
        jnp.bfloat16
    )
    rightward = [(i, i + 1) for i in range(seq_count - 1)]
    leftward = [(i + 1, i) for i in range(seq_count - 1)]
    from_left = lax.ppermute(edge_out[:, BLOCK:], SEQ, rightward).astype(jnp.float32)
    from_right = lax.ppermute(edge_out[:, :BLOCK], SEQ, leftward).astype(jnp.float32)
    global_terms = jnp.sum(global_full, axis=1).astype(jnp.bfloat16)
    global_parts = lax.all_gather(global_terms, SEQ, axis=0)
    accum = wide_grad[:, 1 : block_count + 1]
    accum = accum.at[:, 0].add(from_left)
    accum = accum.at[:, block_count - 1].add(from_right)
    returned = returned.reshape(head_count, seq_count * slot_count, BLOCK * pair_width)
    block_hot = (
        send_block.reshape(-1)[:, None] == jnp.arange(block_count, dtype=jnp.int32)[None, :]
    ) & send_used.reshape(-1)[:, None]
    gathered = jnp.einsum(
        "cb,ecx->ebx", block_hot.astype(jnp.bfloat16), returned, preferred_element_type=jnp.float32
    )
    accum = accum + gathered.reshape(head_count, block_count, BLOCK, pair_width)
    global_sums = jnp.sum(global_parts.astype(jnp.float32), axis=0)
    at_first = (seq_place == 0).astype(jnp.float32)
    accum = accum.at[:, glob_ids].add(global_sums * at_first)
    grad_q = grad_query.reshape(head_count, row_count, head_width).astype(jnp.bfloat16)
    grad_k = accum[..., :head_width].reshape(head_count, row_count, head_width).astype(jnp.bfloat16)
    grad_v = accum[..., head_width:].reshape(head_count, row_count, head_width).astype(jnp.bfloat16)
    return (grad_q, grad_k, grad_v)


def solution(mesh):
    seq_size = mesh.shape["seq"]
    core_size = 2
    devices = mesh.devices.reshape(seq_size // core_size, core_size, mesh.shape["head"])
    split_mesh = Mesh(devices, ("sz", "sc", "head"))
    rows = P("head", SEQ, None)
    return jax.shard_map(
        local,
        mesh=split_mesh,
        in_specs=(rows, rows, rows, rows, P(), P(), P()),
        out_specs=(rows, rows, rows),
        check_vma=False,
    )
```

```python
import math

import jax
import jax.numpy as jnp
from jax import lax
from jax.sharding import PartitionSpec as P

BLOCK = 64


NEG_FILL = -1e30


def local(queries, keys, values, grad_out, rand_owner, rand_slot, glob_ids):
    head_count, row_count, head_width = queries.shape
    block_count = row_count // BLOCK
    rand_count = rand_owner.shape[1]
    glob_count = glob_ids.shape[0]
    seq_count = lax.axis_size("seq")
    seq_place = lax.axis_index("seq")
    slot_count = min(
        block_count, max(2, (2 * block_count * rand_count + seq_count - 1) // seq_count)
    )
    pair_width = 2 * head_width
    score_scale = 1.0 / math.sqrt(head_width)
    paired = jnp.concatenate([keys, values], axis=2)
    paired_blocks = paired.reshape(head_count, block_count, BLOCK, pair_width)
    piece_rows = lax.all_gather(paired, "seq", axis=1, tiled=True)
    row_start = seq_place * row_count
    edge_before = lax.dynamic_slice_in_dim(piece_rows, row_start - BLOCK, BLOCK, axis=1)
    edge_after = lax.dynamic_slice_in_dim(piece_rows, row_start + row_count, BLOCK, axis=1)
    widened = jnp.concatenate([edge_before, paired, edge_after], axis=1)
    widened = widened.reshape(head_count, block_count + 2, BLOCK, pair_width)
    window_pairs = jnp.stack(
        [widened[:, offset : offset + block_count] for offset in range(3)], axis=2
    )
    global_block = seq_place * block_count + jnp.arange(block_count, dtype=jnp.int32)
    window_ids = global_block[:, None] + jnp.arange(-1, 2, dtype=jnp.int32)[None, :]
    window_ok = (window_ids >= 0) & (window_ids < seq_count * block_count)
    owners_all = rand_owner.reshape(seq_count, block_count * rand_count)
    slots_all = rand_slot.reshape(seq_count, block_count * rand_count)
    owner_hot = (
        owners_all[:, :, None] == jnp.arange(seq_count, dtype=jnp.int32)[None, None, :]
    ).astype(jnp.int32)
    before = jnp.cumsum(owner_hot, axis=1) - owner_hot
    position = jnp.sum(before * owner_hot, axis=2)
    to_here = owners_all == seq_place
    slot_hot = (
        position[:, :, None] == jnp.arange(slot_count, dtype=jnp.int32)[None, None, :]
    ) & to_here[:, :, None]
    send_block = jnp.sum(slot_hot.astype(jnp.int32) * slots_all[:, :, None], axis=1)
    send_used = jnp.any(slot_hot, axis=1)
    my_owner = lax.dynamic_index_in_dim(owners_all, seq_place, 0, keepdims=False)
    my_slot = lax.dynamic_index_in_dim(slots_all, seq_place, 0, keepdims=False)
    my_position = lax.dynamic_index_in_dim(position, seq_place, 0, keepdims=False)
    return_at = my_owner * slot_count + my_position
    wanted = my_owner * block_count + my_slot
    piece_blocks = piece_rows.shape[1] // BLOCK
    grouped = piece_rows.reshape(head_count, piece_blocks, BLOCK, pair_width)
    pick_ids = jnp.concatenate([wanted, glob_ids.astype(jnp.int32)])
    picked = jnp.take(grouped, jnp.clip(pick_ids, 0, piece_blocks - 1), axis=1)
    random_pairs = picked[:, : block_count * rand_count].reshape(
        head_count, block_count, rand_count, BLOCK, pair_width
    )
    global_pairs = picked[:, block_count * rand_count :]
    global_wide = jnp.broadcast_to(
        global_pairs[:, None], (head_count, block_count, glob_count, BLOCK, pair_width)
    )
    key_pairs = jnp.concatenate([window_pairs, random_pairs, global_wide], axis=2)
    key_part = key_pairs[..., :head_width]
    value_part = key_pairs[..., head_width:]
    key_valid = jnp.concatenate(
        [window_ok, jnp.ones((block_count, rand_count + glob_count), dtype=bool)], axis=1
    )
    query_blocks = queries.reshape(head_count, block_count, BLOCK, head_width)
    cotan_blocks = grad_out.reshape(head_count, block_count, BLOCK, head_width)
    scores = (
        jnp.einsum("hiqd,hiskd->hiqsk", query_blocks, key_part, preferred_element_type=jnp.float32)
        * score_scale
    )
    scores = jnp.where(key_valid[None, :, None, :, None], scores, NEG_FILL)
    row_max = jnp.max(scores, axis=(3, 4), keepdims=True)
    expo_terms = jnp.exp(scores - row_max)
    weights = expo_terms / jnp.sum(expo_terms, axis=(3, 4), keepdims=True)
    weights_low = weights.astype(jnp.bfloat16)
    attended = jnp.einsum(
        "hiqsk,hiskd->hiqd", weights_low, value_part, preferred_element_type=jnp.float32
    )
    delta = jnp.sum(cotan_blocks.astype(jnp.float32) * attended, axis=3)
    grad_values = jnp.einsum(
        "hiqsk,hiqd->hiskd", weights_low, cotan_blocks, preferred_element_type=jnp.float32
    )
    grad_weights = jnp.einsum(
        "hiqd,hiskd->hiqsk", cotan_blocks, value_part, preferred_element_type=jnp.float32
    )
    grad_scores = (weights * (grad_weights - delta[:, :, :, None, None])).astype(jnp.bfloat16)
    grad_query = (
        jnp.einsum("hiqsk,hiskd->hiqd", grad_scores, key_part, preferred_element_type=jnp.float32)
        * score_scale
    )
    def key_terms(first, last):
        keys_now = jnp.einsum(
            "hiqsk,hiqd->hiskd",
            grad_scores[:, :, :, first:last],
            query_blocks,
            preferred_element_type=jnp.float32,
        )
        values_now = jnp.einsum(
            "hiqsk,hiqd->hiskd",
            weights_low[:, :, :, first:last],
            cotan_blocks,
            preferred_element_type=jnp.float32,
        )
        return jnp.concatenate([keys_now * score_scale, values_now], axis=4)

    random_terms = key_terms(3, 3 + rand_count).astype(jnp.bfloat16)
    random_terms = random_terms.reshape(head_count, block_count * rand_count, BLOCK * pair_width)
    slot_ids = jnp.arange(seq_count * slot_count, dtype=jnp.int32)
    send_hot = slot_ids[:, None] == return_at[None, :]
    outgoing_grads = jnp.einsum(
        "ti,hix->htx", send_hot.astype(jnp.bfloat16), random_terms, preferred_element_type=jnp.float32
    ).astype(jnp.bfloat16)
    outgoing_grads = outgoing_grads.reshape(head_count, seq_count, slot_count, BLOCK, pair_width)
    returned = lax.all_to_all(outgoing_grads, "seq", split_axis=1, concat_axis=1, tiled=True)
    window_terms = key_terms(0, 3)
    global_full = key_terms(3 + rand_count, 3 + rand_count + glob_count)
    wide_grad = jnp.pad(window_terms[:, :, 0], ((0, 0), (0, 2), (0, 0), (0, 0)))
    for offset in range(1, 3):
        wide_grad = wide_grad + jnp.pad(
            window_terms[:, :, offset], ((0, 0), (offset, 2 - offset), (0, 0), (0, 0))
        )
    edge_out = jnp.concatenate([wide_grad[:, 0], wide_grad[:, block_count + 1]], axis=1).astype(
        jnp.bfloat16
    )
    rightward = [(i, i + 1) for i in range(seq_count - 1)]
    leftward = [(i + 1, i) for i in range(seq_count - 1)]
    from_left = lax.ppermute(edge_out[:, BLOCK:], "seq", rightward).astype(jnp.float32)
    from_right = lax.ppermute(edge_out[:, :BLOCK], "seq", leftward).astype(jnp.float32)
    global_terms = jnp.sum(global_full, axis=1).astype(jnp.bfloat16)
    global_parts = lax.all_gather(global_terms, "seq", axis=0)
    accum = wide_grad[:, 1 : block_count + 1]
    accum = accum.at[:, 0].add(from_left)
    accum = accum.at[:, block_count - 1].add(from_right)
    returned = returned.reshape(head_count, seq_count * slot_count, BLOCK * pair_width)
    block_hot = (
        send_block.reshape(-1)[:, None] == jnp.arange(block_count, dtype=jnp.int32)[None, :]
    ) & send_used.reshape(-1)[:, None]
    gathered = jnp.einsum(
        "cb,ecx->ebx", block_hot.astype(jnp.bfloat16), returned, preferred_element_type=jnp.float32
    )
    global_sums = jnp.sum(global_parts.astype(jnp.float32), axis=0)
    at_first = (seq_place == 0).astype(jnp.float32)
    accum = lax.optimization_barrier(accum.at[:, glob_ids].add(global_sums * at_first))
    accum = accum + gathered.reshape(head_count, block_count, BLOCK, pair_width)
    grad_q = grad_query.reshape(head_count, row_count, head_width).astype(jnp.bfloat16)
    grad_k = accum[..., :head_width].reshape(head_count, row_count, head_width).astype(jnp.bfloat16)
    grad_v = accum[..., head_width:].reshape(head_count, row_count, head_width).astype(jnp.bfloat16)
    return (grad_q, grad_k, grad_v)


def solution(mesh):
    return jax.shard_map(
        local,
        mesh=mesh,
        in_specs=(
            P("head", "seq", None),
            P("head", "seq", None),
            P("head", "seq", None),
            P("head", "seq", None),
            P(),
            P(),
            P(),
        ),
        out_specs=(P("head", "seq", None), P("head", "seq", None), P("head", "seq", None)),
        check_vma=False,
    )
```

```python
import math

import jax
import jax.numpy as jnp
from jax import lax
from jax.sharding import PartitionSpec as P

BLOCK = 64


NEG_FILL = -1e30


def local(queries, keys, values, grad_out, rand_owner, rand_slot, glob_ids):
    head_count, row_count, head_width = queries.shape
    block_count = row_count // BLOCK
    rand_count = rand_owner.shape[1]
    glob_count = glob_ids.shape[0]
    seq_count = lax.axis_size("seq")
    seq_place = lax.axis_index("seq")
    slot_count = min(
        block_count, max(2, (2 * block_count * rand_count + seq_count - 1) // seq_count)
    )
    pair_width = 2 * head_width
    score_scale = 1.0 / math.sqrt(head_width)
    paired = jnp.pad(keys, ((0, 0), (0, 0), (0, head_width))) + jnp.pad(
        values, ((0, 0), (0, 0), (head_width, 0))
    )
    paired_blocks = paired.reshape(head_count, block_count, BLOCK, pair_width)
    piece_rows = lax.all_gather(paired, "seq", axis=1, tiled=True)
    row_start = seq_place * row_count
    edge_before = lax.dynamic_slice_in_dim(piece_rows, row_start - BLOCK, BLOCK, axis=1)
    edge_after = lax.dynamic_slice_in_dim(piece_rows, row_start + row_count, BLOCK, axis=1)
    widened = jnp.concatenate([edge_before, paired, edge_after], axis=1)
    widened = widened.reshape(head_count, block_count + 2, BLOCK, pair_width)
    window_pairs = jnp.stack(
        [widened[:, offset : offset + block_count] for offset in range(3)], axis=2
    )
    global_block = seq_place * block_count + jnp.arange(block_count, dtype=jnp.int32)
    window_ids = global_block[:, None] + jnp.arange(-1, 2, dtype=jnp.int32)[None, :]
    window_ok = (window_ids >= 0) & (window_ids < seq_count * block_count)
    owners_all = rand_owner.reshape(seq_count, block_count * rand_count)
    slots_all = rand_slot.reshape(seq_count, block_count * rand_count)
    owner_hot = (
        owners_all[:, :, None] == jnp.arange(seq_count, dtype=jnp.int32)[None, None, :]
    ).astype(jnp.int32)
    before = jnp.cumsum(owner_hot, axis=1) - owner_hot
    position = jnp.sum(before * owner_hot, axis=2)
    to_here = owners_all == seq_place
    slot_hot = (
        position[:, :, None] == jnp.arange(slot_count, dtype=jnp.int32)[None, None, :]
    ) & to_here[:, :, None]
    send_block = jnp.sum(slot_hot.astype(jnp.int32) * slots_all[:, :, None], axis=1)
    send_used = jnp.any(slot_hot, axis=1)
    my_owner = lax.dynamic_index_in_dim(owners_all, seq_place, 0, keepdims=False)
    my_slot = lax.dynamic_index_in_dim(slots_all, seq_place, 0, keepdims=False)
    my_position = lax.dynamic_index_in_dim(position, seq_place, 0, keepdims=False)
    return_at = my_owner * slot_count + my_position
    wanted = my_owner * block_count + my_slot
    piece_blocks = piece_rows.shape[1] // BLOCK
    grouped = piece_rows.reshape(head_count, piece_blocks, BLOCK, pair_width)
    pick_ids = jnp.concatenate([wanted, glob_ids.astype(jnp.int32)])
    picked = jnp.take(grouped, jnp.clip(pick_ids, 0, piece_blocks - 1), axis=1)
    random_pairs = picked[:, : block_count * rand_count].reshape(
        head_count, block_count, rand_count, BLOCK, pair_width
    )
    global_pairs = picked[:, block_count * rand_count :]
    global_wide = jnp.broadcast_to(
        global_pairs[:, None], (head_count, block_count, glob_count, BLOCK, pair_width)
    )
    key_pairs = jnp.concatenate([window_pairs, random_pairs, global_wide], axis=2)
    key_part = key_pairs[..., :head_width]
    value_part = key_pairs[..., head_width:]
    key_valid = jnp.concatenate(
        [window_ok, jnp.ones((block_count, rand_count + glob_count), dtype=bool)], axis=1
    )
    query_blocks = queries.reshape(head_count, block_count, BLOCK, head_width)
    cotan_blocks = grad_out.reshape(head_count, block_count, BLOCK, head_width)
    scores = (
        jnp.einsum("hiqd,hiskd->hiqsk", query_blocks, key_part, preferred_element_type=jnp.float32)
        * score_scale
    )
    scores = jnp.where(key_valid[None, :, None, :, None], scores, NEG_FILL)
    row_max = jnp.max(scores, axis=(3, 4), keepdims=True)
    expo_terms = jnp.exp(scores - row_max)
    weights = expo_terms / jnp.sum(expo_terms, axis=(3, 4), keepdims=True)
    weights_low = weights.astype(jnp.bfloat16)
    attended = jnp.einsum(
        "hiqsk,hiskd->hiqd", weights_low, value_part, preferred_element_type=jnp.float32
    )
    delta = jnp.sum(cotan_blocks.astype(jnp.float32) * attended, axis=3)
    grad_values = jnp.einsum(
        "hiqsk,hiqd->hiskd", weights_low, cotan_blocks, preferred_element_type=jnp.float32
    )
    grad_weights = jnp.einsum(
        "hiqd,hiskd->hiqsk", cotan_blocks, value_part, preferred_element_type=jnp.float32
    )
    grad_scores = (weights * (grad_weights - delta[:, :, :, None, None])).astype(jnp.bfloat16)
    grad_query = (
        jnp.einsum("hiqsk,hiskd->hiqd", grad_scores, key_part, preferred_element_type=jnp.float32)
        * score_scale
    )
    def key_terms(first, last):
        keys_now = jnp.einsum(
            "hiqsk,hiqd->hiskd",
            grad_scores[:, :, :, first:last],
            query_blocks,
            preferred_element_type=jnp.float32,
        )
        values_now = jnp.einsum(
            "hiqsk,hiqd->hiskd",
            weights_low[:, :, :, first:last],
            cotan_blocks,
            preferred_element_type=jnp.float32,
        )
        return jnp.concatenate([keys_now * score_scale, values_now], axis=4)

    random_terms = key_terms(3, 3 + rand_count).astype(jnp.bfloat16)
    random_terms = random_terms.reshape(head_count, block_count * rand_count, BLOCK * pair_width)
    slot_ids = jnp.arange(seq_count * slot_count, dtype=jnp.int32)
    send_hot = slot_ids[:, None] == return_at[None, :]
    outgoing_grads = jnp.einsum(
        "ti,hix->htx", send_hot.astype(jnp.bfloat16), random_terms, preferred_element_type=jnp.float32
    ).astype(jnp.bfloat16)
    outgoing_grads = outgoing_grads.reshape(head_count, seq_count, slot_count, BLOCK, pair_width)
    returned = lax.all_to_all(outgoing_grads, "seq", split_axis=1, concat_axis=1, tiled=True)
    window_terms = key_terms(0, 3)
    global_full = key_terms(3 + rand_count, 3 + rand_count + glob_count)
    wide_grad = jnp.pad(window_terms[:, :, 0], ((0, 0), (0, 2), (0, 0), (0, 0)))
    for offset in range(1, 3):
        wide_grad = wide_grad + jnp.pad(
            window_terms[:, :, offset], ((0, 0), (offset, 2 - offset), (0, 0), (0, 0))
        )
    edge_out = jnp.concatenate([wide_grad[:, 0], wide_grad[:, block_count + 1]], axis=1).astype(
        jnp.bfloat16
    )
    rightward = [(i, i + 1) for i in range(seq_count - 1)]
    leftward = [(i + 1, i) for i in range(seq_count - 1)]
    from_left = lax.ppermute(edge_out[:, BLOCK:], "seq", rightward).astype(jnp.float32)
    from_right = lax.ppermute(edge_out[:, :BLOCK], "seq", leftward).astype(jnp.float32)
    global_terms = jnp.sum(global_full, axis=1).astype(jnp.bfloat16)
    global_parts = lax.all_gather(global_terms, "seq", axis=0)
    accum = wide_grad[:, 1 : block_count + 1]
    accum = accum.at[:, 0].add(from_left)
    accum = accum.at[:, block_count - 1].add(from_right)
    returned = returned.reshape(head_count, seq_count * slot_count, BLOCK * pair_width)
    block_hot = (
        send_block.reshape(-1)[:, None] == jnp.arange(block_count, dtype=jnp.int32)[None, :]
    ) & send_used.reshape(-1)[:, None]
    gathered = jnp.einsum(
        "cb,ecx->ebx", block_hot.astype(jnp.bfloat16), returned, preferred_element_type=jnp.float32
    )
    accum = accum + gathered.reshape(head_count, block_count, BLOCK, pair_width)
    global_sums = jnp.sum(global_parts.astype(jnp.float32), axis=0)
    at_first = (seq_place == 0).astype(jnp.float32)
    accum = accum.at[:, glob_ids].add(global_sums * at_first)
    grad_q = grad_query.reshape(head_count, row_count, head_width).astype(jnp.bfloat16)
    grad_k = accum[..., :head_width].reshape(head_count, row_count, head_width).astype(jnp.bfloat16)
    grad_v = accum[..., head_width:].reshape(head_count, row_count, head_width).astype(jnp.bfloat16)
    return (grad_q, grad_k, grad_v)


def solution(mesh):
    return jax.shard_map(
        local,
        mesh=mesh,
        in_specs=(
            P("head", "seq", None),
            P("head", "seq", None),
            P("head", "seq", None),
            P("head", "seq", None),
            P(),
            P(),
            P(),
        ),
        out_specs=(P("head", "seq", None), P("head", "seq", None), P("head", "seq", None)),
        check_vma=False,
    )
```
